128 devices in a mesh: seq: 64 (over z, x, y), tp: 2 (over core).
Axes of the slice: x: 4, y: 4, z: 4, core: 2. Of those that a mesh axis runs over, the one named last changes fastest.
Arguments:
- layer_input: bfloat16 [16384, 2048], P('seq'), may hold values from -1.5 to 1.5
- query: bfloat16 [16384, 2048], P('seq', 'tp'), may hold values from -6 to 6
- suffix_kv: bfloat16 [2, 16384, 2048], P(None, 'seq', 'tp'), may hold values from -6 to 6
- prefix_kv: bfloat16 [2, 2048, 2048], P(None, 'seq', 'tp'), may hold values from -6 to 6
- node_len: int32 [64], replicated, may hold values from 8 to 32, as said below
- path: int32 [64, 3], P('seq'), may hold values from 0 to 63, as said below
- out_weight: bfloat16 [2048, 2048], P('tp'), may hold values from -0.125 to 0.125
- norm_gain: float32 [2048], replicated, may hold values from 0.1 to 1.9
- expert_ids: int32 [16384, 8], P('seq'), may hold values from 0 to 63, all different within a row; in each aligned block of 256 rows (0 to 255, 256 to 511, ...) at most 40 rows name the same one
- gates: float32 [16384, 8], P('seq'), may hold values from 0.1 to 0.4
- w_gate: bfloat16 [64, 2048, 1024], P('seq', None, 'tp'), may hold values from -0.125 to 0.125
- w_up: bfloat16 [64, 2048, 1024], P('seq', None, 'tp'), may hold values from -0.125 to 0.125
- w_down: bfloat16 [64, 1024, 2048], P('seq', 'tp'), may hold values from -0.1875 to 0.1875
Outputs:
- layer_out: bfloat16 [16384, 2048], P('seq', 'tp')
The draws below stay inside these ranges and needn't reach their ends.
Inputs may be any that keep to these rules, and one draw needn't show every extreme that they name: `path`: row r names three different nodes. Nodes are of three levels: roots, middle nodes and leaves; a middle node always comes with the same root, a leaf always with the same middle node, and every node is named by some request. `node_len`: some node holds exactly 32 tokens. `expert_ids`: within the 256 rows of one request no expert is named more than 40 times, a bound that some block reaches.
All inputs are finite; a program needn't handle non-finite values.
Results may differ from the reference program's by a relative error of at most 0.019.
Values may be sent and summed in bfloat16 or wider, within the bound.
No kernel may reach another device: no remote copies, remote signals or barrier semaphores. Data moves between devices by JAX's collectives and lax.ppermute only.
A program may use at most 128 MiB of HBM per device.

```python
import math
import jax
import jax.numpy as jnp
import numpy as np
from jax import lax

D = 2048
HEADS = 16
HD = 128
FF = 1024
TOPK = 8
Q = 256
SLOT = 32
EXPERTS = 64
NODES = 64
REQ = 64
TOKENS = 16384
CAP = 40


def draw_query(key, part):
    base = jnp.clip(jax.random.normal(jax.random.fold_in(key, 1), (TOKENS, HEADS * HD), jnp.float32), -4.0, 4.0)
    return base.astype(jnp.bfloat16)


def draw_suffix_kv(key, part):
    base = jnp.clip(jax.random.normal(jax.random.fold_in(key, 3), (2, TOKENS, HEADS * HD), jnp.float32), -4.0, 4.0)
    return base.astype(jnp.bfloat16)


def draw_node_len(key, part):
    lens = jax.random.randint(jax.random.fold_in(key, 31), (NODES,), SLOT // 4, SLOT + 1)
    full = jax.random.randint(jax.random.fold_in(key, 32), (), 0, NODES)
    return jnp.where(jnp.arange(NODES) == full, SLOT, lens).astype(jnp.int32)


def draw_path(key, part):
    roots = NODES // 16
    middles = 3 * NODES // 16
    leaves = 12 * NODES // 16
    owner = jax.random.permutation(jax.random.fold_in(key, 21), NODES)
    extra = jax.random.randint(jax.random.fold_in(key, 23), (REQ - leaves,), 0, leaves)
    leaf_of = jnp.concatenate([jnp.arange(leaves), extra])
    order = jax.random.permutation(jax.random.fold_in(key, 22), REQ)
    leaf_of = leaf_of[order]
    middle_of = leaf_of // 4
    root_of = middle_of // 3
    return jnp.stack([owner[root_of], owner[roots + middle_of], owner[roots + middles + leaf_of]], 1).astype(jnp.int32)


def block_scale(own_key, shape, split, smallest, largest):
    def one(position, shards_of):
        steps = jax.random.uniform(jax.random.fold_in(jax.random.fold_in(own_key, 6), position), (shards_of,), jnp.float32, smallest / len(split), largest / len(split))
        return jnp.repeat(jnp.exp(steps), shape[position] // shards_of).reshape((-1,) + (1,) * (len(shape) - position - 1))

    loudness = one(*split[0])
    for cut in split[1:]:
        loudness = loudness * one(*cut)
    return loudness


def shared_out(rng, own, number, rows, count, top, bound, lean):
    sequence = jax.random.permutation(rng, count)
    packed, usual = load_shares(count, rows * top, bound, lean, True), load_shares(count, rows * top, bound, lean, False)
    places = jnp.arange(count)

    def named(lengths, turn):
        used = int((lengths > 0).sum())
        fixed = max(1, used // 4)
        shifted = fixed + (places - fixed + turn * (used - fixed)) % max(1, count - fixed)
        return jnp.zeros((count,), jnp.int32).at[sequence[jnp.where(places < fixed, places, shifted)]].set(jnp.asarray(lengths, jnp.int32))

    lengths = jnp.where(number % 4 == 0, named(packed, number // 4), named(usual, number - number // 4 - 1))
    mixed = jax.random.permutation(jax.random.fold_in(own, 3), count)
    giver, receiver = mixed[0:count // 2 * 2:2], mixed[1:count // 2 * 2:2]
    margin = jnp.minimum(lengths[giver] - 1, bound - lengths[receiver]) // 2
    margin = jnp.where((giver == sequence[0]) | (receiver == sequence[0]) | (lengths[receiver] == 0), 0, jnp.maximum(margin, 0))
    shifted = jax.random.randint(jax.random.fold_in(own, 4), (count // 2,), 0, 1 << 20) % (margin + 1)
    lengths = lengths.at[giver].add(-shifted).at[receiver].add(shifted)
    labels = jnp.searchsorted(jnp.cumsum(lengths), jnp.arange(rows * top), side="right").astype(jnp.int32)
    listing = labels.reshape(top, rows).T
    listing = listing[jax.random.permutation(jax.random.fold_in(own, 1), rows)]
    turn = jax.random.randint(jax.random.fold_in(own, 2), (rows, 1), 0, top)
    return jnp.take_along_axis(listing, (jnp.arange(top)[None, :] + turn) % top, axis=1)


def load_shares(number_of, total, bound, skew, full):
    weights = [(1 << 20) // math.isqrt(rank ** skew) + 1 for rank in range(1, number_of + 1)]
    largest = bound if full else min(bound, max(-(-total // number_of), total * weights[0] // sum(weights)))
    least = 1 if total - largest >= number_of - 1 else 0
    given, rest = [largest] + [least] * (number_of - 1), total - largest - least * (number_of - 1)
    while rest > 0:
        free = [i for i in range(1, number_of) if given[i] < largest] or [i for i in range(1, number_of) if given[i] < bound]
        pool, left = sum([weights[i] for i in free]), rest
        for i in free:
            more = min(bound - given[i], max(1, left * weights[i] // pool), rest)
            given[i] = given[i] + more
            rest = rest - more
    return np.array(given)


def centred(key, shape, scale, bound, split=(), held_as=jnp.bfloat16):
    gain = block_scale(key, shape, split, -0.22, 0.18) if split else 1.0
    entries = jax.random.normal(key, shape, jnp.float32) * scale * gain
    return jnp.minimum(jnp.maximum(entries, -bound), bound).astype(held_as)


def setup_inputs(seed: int = 0) -> dict:
    key_list = jax.random.split(jax.random.key(seed), 14)
    layer_input = centred(key_list[0], (TOKENS, D), 0.25, 1.5, ((0, 64),))
    query = draw_query(jax.random.fold_in(key_list[13], 71), 0)
    suffix_kv = draw_suffix_kv(jax.random.fold_in(key_list[13], 71), 0)
    prefix_kv = centred(key_list[3], (2, NODES * SLOT, HEADS * HD), 1.0, 6.0, ((1, 64), (2, 2)))
    node_len = draw_node_len(jax.random.fold_in(key_list[13], 71), 0)
    path = draw_path(jax.random.fold_in(key_list[13], 71), 0)
    out_weight = centred(key_list[6], (HEADS * HD, D), (HEADS * HD) ** -0.5, 0.125, ((0, 2),))
    norm_gain = jnp.clip(1.0 + 0.18 * jax.random.normal(key_list[7], (D,), jnp.float32), 0.1, 1.9)
    expert_ids_keys = jax.random.split(jax.random.fold_in(key_list[8], 1), TOKENS // Q)
    expert_ids_turns = jax.random.permutation(jax.random.fold_in(key_list[8], 3), TOKENS // Q)
    expert_ids = jax.vmap(lambda own, number: shared_out(jax.random.fold_in(key_list[8], 2), own, number, Q, EXPERTS, TOPK, CAP, 2))(expert_ids_keys, expert_ids_turns).reshape((TOKENS, TOPK))
    gates = jnp.clip(0.1 + 0.3 * jax.random.uniform(key_list[9], (TOKENS, TOPK), jnp.float32) ** block_scale(key_list[9], (TOKENS, TOPK), ((0, 64),), -0.2, 0.2), 0.1, 0.4)
    w_gate = centred(key_list[10], (EXPERTS, D, FF), D ** -0.5, 0.125, ((0, 64), (2, 2)))
    w_up = centred(key_list[11], (EXPERTS, D, FF), D ** -0.5, 0.125, ((0, 64), (2, 2)))
    w_down = centred(key_list[12], (EXPERTS, FF, D), FF ** -0.5, 0.1875, ((0, 64), (1, 2)))
    return dict(layer_input=layer_input, query=query, suffix_kv=suffix_kv, prefix_kv=prefix_kv, node_len=node_len, path=path, out_weight=out_weight, norm_gain=norm_gain, expert_ids=expert_ids, gates=gates, w_gate=w_gate, w_up=w_up, w_down=w_down)


def slot_plan(ids, experts, cap):
    flat = ids.reshape(-1)
    onehot = (flat[:, None] == jnp.arange(experts, dtype=jnp.int32)[None, :]).astype(jnp.int32)
    rank = lax.optimization_barrier(jnp.sum(jnp.cumsum(onehot, axis=0) * onehot, axis=1)) - 1
    return (flat * cap + rank).astype(jnp.int32)

def reference(layer_input, query, suffix_kv, prefix_kv, node_len, path, out_weight, norm_gain, expert_ids, gates, w_gate, w_up, w_down):
    width = HEADS * HD
    scale = 1.0 / math.sqrt(HD)
    prefix = prefix_kv.reshape(2, NODES, SLOT, width)
    positions = jnp.arange(SLOT, dtype=jnp.int32)

    def attend(item):
        queries, own_kv, nodes = item
        node_keys = prefix[0][nodes].reshape(3 * SLOT, width)
        node_values = prefix[1][nodes].reshape(3 * SLOT, width)
        live = (positions[None, :] < node_len[nodes][:, None]).reshape(-1)
        live_all = jnp.concatenate([jnp.ones((Q,), dtype=bool), live])
        keys = jnp.concatenate([own_kv[0], node_keys], 0).astype(jnp.float32).reshape(-1, HEADS, HD)
        values = jnp.concatenate([own_kv[1], node_values], 0).astype(jnp.float32).reshape(-1, HEADS, HD)
        scores = jnp.einsum('qhd,khd->hqk', queries.astype(jnp.float32).reshape(Q, HEADS, HD), keys) * scale
        scores = jnp.where(live_all[None, None, :], scores, -jnp.inf)
        weights = jax.nn.softmax(scores, axis=2)
        result = jnp.einsum('hqk,khd->qhd', weights, values)
        return result.reshape(Q, width).astype(jnp.bfloat16)
    blocks = (query.reshape(REQ, Q, width), suffix_kv.reshape(2, REQ, Q, width).transpose(1, 0, 2, 3), path)
    attn = lax.map(attend, blocks).reshape(TOKENS, width)
    hidden_state = layer_input.astype(jnp.float32) + jnp.dot(attn, out_weight, preferred_element_type=jnp.float32)
    mean_square = lax.optimization_barrier(jnp.mean(hidden_state * hidden_state, axis=1, keepdims=True))
    normed = (hidden_state * lax.rsqrt(mean_square + 1e-06) * norm_gain).astype(jnp.bfloat16)
    dest = jax.vmap(lambda ids: slot_plan(ids, EXPERTS, CAP))(expert_ids.reshape(REQ, Q, TOPK))
    pairs_all = TOKENS * TOPK
    pair_index = jnp.arange(pairs_all, dtype=jnp.int32).reshape(REQ, Q * TOPK)
    table = jnp.full((REQ, EXPERTS * CAP), pairs_all, dtype=jnp.int32)
    table = table.at[jnp.arange(REQ, dtype=jnp.int32)[:, None], dest].set(pair_index)
    table = table.reshape(REQ, EXPERTS, CAP).transpose(1, 0, 2).reshape(EXPERTS, REQ * CAP)
    gate_flat = gates.reshape(-1)

    def add_expert(accum, item):
        gate_w, up_w, down_w, pairs = item
        valid = pairs < pairs_all
        safe = jnp.minimum(pairs, pairs_all - 1)
        token = (safe // TOPK).astype(jnp.int32)
        rows = normed[token]
        gate_part = jnp.dot(rows, gate_w, preferred_element_type=jnp.float32)
        up_part = jnp.dot(rows, up_w, preferred_element_type=jnp.float32)
        act = (jax.nn.silu(gate_part) * up_part).astype(jnp.bfloat16)
        result = jnp.dot(act, down_w, preferred_element_type=jnp.float32).astype(jnp.bfloat16)
        result = lax.optimization_barrier(result).astype(jnp.float32)
        weight = jnp.where(valid, gate_flat[safe], jnp.zeros_like(gate_flat[safe]))
        return (accum.at[token].add(weight[:, None] * result), None)
    accum, _ = lax.scan(add_expert, jnp.zeros((TOKENS, D), jnp.float32), (w_gate, w_up, w_down, table))
    return (hidden_state + accum).astype(jnp.bfloat16)
```

```python
import math

import jax
import jax.numpy as jnp
from jax import lax
from jax.sharding import PartitionSpec as P

D = 2048
HD = 128
TOPK = 8


def local(
    layer_input,
    query,
    suffix_kv,
    prefix_kv,
    node_len,
    path,
    out_weight,
    norm_gain,
    expert_ids,
    gates,
    w_gate,
    w_up,
    w_down,
):
    rows = query.shape[0]
    width = query.shape[1]
    heads_here = width // HD
    scale = 1.0 / math.sqrt(HD)
    seq_count = lax.axis_size("seq")
    tp_index = lax.axis_index("tp")
    tp_count = lax.axis_size("tp")
    depth = path.shape[1]
    slot = prefix_kv.shape[1]

    gate_full = lax.all_gather(w_gate[0], "tp", axis=1, tiled=True)
    up_full = lax.all_gather(w_up[0], "tp", axis=1, tiled=True)
    down_full = lax.all_gather(w_down[0], "tp", axis=0, tiled=True)

    pieces = prefix_kv.reshape(seq_count, -1)
    piece = pieces.shape[1]
    spread = lax.all_to_all(pieces, "seq", 0, 0, tiled=True)
    paths = lax.all_to_all(
        jnp.broadcast_to(path, (seq_count, depth)), "seq", 0, 0, tiled=True
    )
    node_ids = jnp.arange(spread.shape[0], dtype=jnp.int32)
    pick = (paths.reshape(-1)[:, None] == node_ids[None, :]).astype(spread.dtype)
    picked = jnp.dot(pick, spread, preferred_element_type=jnp.float32).astype(spread.dtype)
    got = lax.all_to_all(picked.reshape(seq_count, depth * piece), "seq", 0, 0, tiled=True)
    nodes_kv = got.reshape(seq_count, depth, piece).transpose(1, 0, 2).reshape(depth, 2, slot, width)
    prefix_keys = nodes_kv[:, 0].reshape(depth * slot, heads_here, HD)
    prefix_values = nodes_kv[:, 1].reshape(depth * slot, heads_here, HD)

    my_nodes = path[0]
    lengths = jnp.sum(
        jnp.where(my_nodes[:, None] == node_ids[None, :], node_len[None, :], 0), axis=1
    )
    live = (jnp.arange(slot, dtype=jnp.int32)[None, :] < lengths[:, None]).reshape(-1)
    live_all = jnp.concatenate([jnp.ones((rows,), dtype=bool), live])

    queries = query.reshape(rows, heads_here, HD)
    keys = jnp.concatenate([suffix_kv[0].reshape(rows, heads_here, HD), prefix_keys], 0)
    values = jnp.concatenate(
        [suffix_kv[1].reshape(rows, heads_here, HD), prefix_values], 0
    ).astype(jnp.float32)
    scores = (
        jnp.einsum("qhd,khd->hqk", queries, keys, preferred_element_type=jnp.float32) * scale
    )
    scores = jnp.where(live_all[None, None, :], scores, -jnp.inf)
    top = jnp.max(scores, axis=2)
    probs = jnp.exp(scores - top[:, :, None])
    total = jnp.sum(probs, axis=2)
    accum = jnp.einsum("hqk,khd->hqd", probs, values)
    attn = (accum / total[:, :, None]).astype(jnp.bfloat16)
    partial_value = jnp.einsum(
        "hqd,hdm->qm",
        attn,
        out_weight.reshape(heads_here, HD, D),
        preferred_element_type=jnp.float32,
    )
    hidden_state = layer_input.astype(jnp.float32) + lax.psum(partial_value, "tp")
    mean_square = jnp.mean(hidden_state * hidden_state, axis=1, keepdims=True)
    normed = (hidden_state * lax.rsqrt(mean_square + 1e-06) * norm_gain).astype(jnp.bfloat16)

    experts = w_gate.shape[0] * seq_count
    cap = 5 * rows * TOPK // (4 * experts)
    share = cap // tp_count
    hit = expert_ids[:, :, None] == jnp.arange(experts, dtype=jnp.int32)[None, None, :]
    chosen = jnp.any(hit, axis=1)
    weight_of = jnp.sum(jnp.where(hit, gates[:, :, None], 0.0), axis=1)
    token = jnp.arange(rows, dtype=jnp.int32)
    earlier = (token[None, :] < token[:, None]).astype(jnp.bfloat16)
    ranks = jnp.dot(
        earlier, chosen.astype(jnp.bfloat16), preferred_element_type=jnp.float32
    ).astype(jnp.int32)
    target = tp_index * share + jnp.arange(share, dtype=jnp.int32)
    sel = chosen[:, :, None] & (ranks[:, :, None] == target[None, None, :])
    sel = sel.reshape(rows, experts * share)
    outgoing = jnp.einsum(
        "ts,td->sd", sel.astype(jnp.bfloat16), normed, preferred_element_type=jnp.float32
    ).astype(jnp.bfloat16)
    arrived = lax.all_to_all(
        outgoing.reshape(experts, share, D), "seq", 0, 0, tiled=True
    ).reshape(experts * share, D)
    gate_part = jnp.dot(arrived, gate_full, preferred_element_type=jnp.float32)
    up_part = jnp.dot(arrived, up_full, preferred_element_type=jnp.float32)
    act = (jax.nn.silu(gate_part) * up_part).astype(jnp.bfloat16)
    result = jnp.dot(act, down_full, preferred_element_type=jnp.float32).astype(jnp.bfloat16)
    back = lax.all_to_all(result.reshape(experts, share, D), "seq", 0, 0, tiled=True)
    back = back.reshape(experts * share, D)

    combine = jnp.where(sel, jnp.repeat(weight_of, share, axis=1), 0.0)
    combine_hi = combine.astype(jnp.bfloat16)
    combine_lo = (combine - combine_hi.astype(jnp.float32)).astype(jnp.bfloat16)
    mixture = jnp.dot(combine_hi, back, preferred_element_type=jnp.float32) + jnp.dot(
        combine_lo, back, preferred_element_type=jnp.float32
    )
    mixture = lax.psum_scatter(mixture, "tp", scatter_dimension=1, tiled=True)
    half = D // tp_count
    residual = lax.dynamic_slice_in_dim(hidden_state, tp_index * half, half, 1)
    return (residual + mixture).astype(jnp.bfloat16)


def solution(mesh):
    in_specs = (
        P("seq", None),
        P("seq", "tp"),
        P(None, "seq", "tp"),
        P(None, "seq", "tp"),
        P(),
        P("seq", None),
        P("tp", None),
        P(),
        P("seq", None),
        P("seq", None),
        P("seq", None, "tp"),
        P("seq", None, "tp"),
        P("seq", "tp", None),
    )
    out_specs = P("seq", "tp")
    return jax.shard_map(local, mesh=mesh, in_specs=in_specs, out_specs=out_specs, check_vma=False)
```

```python
import math

import jax
import jax.numpy as jnp
from jax import lax
from jax.sharding import PartitionSpec as P

D = 2048
HD = 128
TOPK = 8


def local(
    layer_input,
    query,
    suffix_kv,
    prefix_kv,
    node_len,
    path,
    out_weight,
    norm_gain,
    expert_ids,
    gates,
    w_gate,
    w_up,
    w_down,
):
    rows = query.shape[0]
    width = query.shape[1]
    heads_here = width // HD
    scale = 1.0 / math.sqrt(HD)
    seq_count = lax.axis_size("seq")
    tp_index = lax.axis_index("tp")
    tp_count = lax.axis_size("tp")
    depth = path.shape[1]
    slot = prefix_kv.shape[1]

    gate_full = lax.all_gather(w_gate[0], "tp", axis=1, tiled=True)
    up_full = lax.all_gather(w_up[0], "tp", axis=1, tiled=True)
    down_full = lax.all_gather(w_down[0], "tp", axis=0, tiled=True)

    pieces = prefix_kv.reshape(seq_count, -1)
    piece = pieces.shape[1]
    tag = jnp.zeros((seq_count, 128), pieces.dtype).at[:, :depth].set(
        jnp.broadcast_to(path.astype(pieces.dtype), (seq_count, depth))
    )
    spread = lax.all_to_all(jnp.concatenate([pieces, tag], 1), "seq", 0, 0, tiled=True)
    paths = spread[:, piece : piece + depth].astype(jnp.int32)
    spread = spread[:, :piece]
    node_ids = jnp.arange(spread.shape[0], dtype=jnp.int32)
    pick = (paths.reshape(-1)[:, None] == node_ids[None, :]).astype(spread.dtype)
    picked = jnp.dot(pick, spread, preferred_element_type=jnp.float32).astype(spread.dtype)
    got = lax.all_to_all(picked.reshape(seq_count, depth * piece), "seq", 0, 0, tiled=True)
    nodes_kv = got.reshape(seq_count, depth, piece).transpose(1, 0, 2).reshape(depth, 2, slot, width)
    prefix_keys = nodes_kv[:, 0].reshape(depth * slot, heads_here, HD)
    prefix_values = nodes_kv[:, 1].reshape(depth * slot, heads_here, HD)

    my_nodes = path[0]
    lengths = jnp.sum(
        jnp.where(my_nodes[:, None] == node_ids[None, :], node_len[None, :], 0), axis=1
    )
    live = (jnp.arange(slot, dtype=jnp.int32)[None, :] < lengths[:, None]).reshape(-1)
    live_all = jnp.concatenate([jnp.ones((rows,), dtype=bool), live])

    queries = query.reshape(rows, heads_here, HD)
    keys = jnp.concatenate([suffix_kv[0].reshape(rows, heads_here, HD), prefix_keys], 0)
    values = jnp.concatenate(
        [suffix_kv[1].reshape(rows, heads_here, HD), prefix_values], 0
    ).astype(jnp.float32)
    scores = (
        jnp.einsum("qhd,khd->hqk", queries, keys, preferred_element_type=jnp.float32) * scale
    )
    scores = jnp.where(live_all[None, None, :], scores, -jnp.inf)
    top = jnp.max(scores, axis=2)
    probs = jnp.exp(scores - top[:, :, None])
    total = jnp.sum(probs, axis=2)
    accum = jnp.einsum("hqk,khd->hqd", probs, values)
    attn = (accum / total[:, :, None]).astype(jnp.bfloat16)
    partial_value = jnp.einsum(
        "hqd,hdm->qm",
        attn,
        out_weight.reshape(heads_here, HD, D),
        preferred_element_type=jnp.float32,
    )
    hidden_state = layer_input.astype(jnp.float32) + lax.psum(partial_value, "tp")
    mean_square = jnp.mean(hidden_state * hidden_state, axis=1, keepdims=True)
    normed = (hidden_state * lax.rsqrt(mean_square + 1e-06) * norm_gain).astype(jnp.bfloat16)

    experts = w_gate.shape[0] * seq_count
    cap = 5 * rows * TOPK // (4 * experts)
    share = -(-(-(-cap // tp_count)) // 8) * 8
    hit = expert_ids[:, :, None] == jnp.arange(experts, dtype=jnp.int32)[None, None, :]
    chosen = jnp.any(hit, axis=1)
    weight_of = jnp.sum(jnp.where(hit, gates[:, :, None], 0.0), axis=1)
    token = jnp.arange(rows, dtype=jnp.int32)
    earlier = (token[None, :] < token[:, None]).astype(jnp.bfloat16)
    ranks = jnp.dot(
        earlier, chosen.astype(jnp.bfloat16), preferred_element_type=jnp.float32
    ).astype(jnp.int32)
    target = tp_count * jnp.arange(share, dtype=jnp.int32) + tp_index
    sel = chosen[:, :, None] & (ranks[:, :, None] == target[None, None, :])
    sel = sel.reshape(rows, experts * share).astype(jnp.bfloat16)
    outgoing = jnp.einsum(
        "ts,td->sd", sel, normed, preferred_element_type=jnp.float32
    ).astype(jnp.bfloat16)
    arrived = lax.all_to_all(
        outgoing.reshape(experts, share, D), "seq", 0, 0, tiled=True
    ).reshape(experts * share, D)
    gate_part = jnp.dot(arrived, gate_full, preferred_element_type=jnp.float32)
    up_part = jnp.dot(arrived, up_full, preferred_element_type=jnp.float32)
    act = (jax.nn.silu(gate_part) * up_part).astype(jnp.bfloat16)
    half = D // tp_count
    result = jnp.einsum(
        "sf,fuc->usc",
        act,
        down_full.reshape(down_full.shape[0], tp_count, half),
        preferred_element_type=jnp.float32,
    ).astype(jnp.bfloat16)
    back = lax.all_to_all(
        result.reshape(tp_count * experts, share, half), ("tp", "seq"), 0, 0, tiled=True
    )
    back = back.reshape(tp_count * experts * share, half)

    spot = (
        tp_count * jnp.arange(share, dtype=jnp.int32)[None, None, :]
        + jnp.arange(tp_count, dtype=jnp.int32)[:, None, None]
    )
    combine = jnp.where(
        chosen.T[None, :, :, None] & (ranks.T[None, :, :, None] == spot[:, None, :, :]),
        weight_of.T[None, :, :, None],
        0.0,
    )
    combine = jnp.moveaxis(combine, 2, 0).reshape(rows, -1)
    combine_hi = combine.astype(jnp.bfloat16)
    combine_lo = (combine - combine_hi.astype(jnp.float32)).astype(jnp.bfloat16)
    combine_hi, combine_lo = lax.optimization_barrier((combine_hi, combine_lo))
    mixture = jnp.dot(combine_hi, back, preferred_element_type=jnp.float32) + jnp.dot(
        combine_lo, back, preferred_element_type=jnp.float32
    )
    residual = lax.dynamic_slice_in_dim(hidden_state, tp_index * half, half, 1)
    return (residual + mixture).astype(jnp.bfloat16)


def solution(mesh):
    in_specs = (
        P("seq", None),
        P("seq", "tp"),
        P(None, "seq", "tp"),
        P(None, "seq", "tp"),
        P(),
        P("seq", None),
        P("tp", None),
        P(),
        P("seq", None),
        P("seq", None),
        P("seq", None, "tp"),
        P("seq", None, "tp"),
        P("seq", "tp", None),
    )
    out_specs = P("seq", "tp")
    return jax.shard_map(local, mesh=mesh, in_specs=in_specs, out_specs=out_specs, check_vma=False)
```

```python
import math

import jax
import jax.numpy as jnp
from jax import lax
from jax.sharding import PartitionSpec as P

D = 2048
HD = 128
TOPK = 8


def local(
    layer_input,
    query,
    suffix_kv,
    prefix_kv,
    node_len,
    path,
    out_weight,
    norm_gain,
    expert_ids,
    gates,
    w_gate,
    w_up,
    w_down,
):
    rows = query.shape[0]
    width = query.shape[1]
    heads_here = width // HD
    scale = 1.0 / math.sqrt(HD)
    seq_count = lax.axis_size("seq")
    tp_index = lax.axis_index("tp")
    tp_count = lax.axis_size("tp")
    depth = path.shape[1]
    slot = prefix_kv.shape[1]

    swap = [(i, (i + 1) % tp_count) for i in range(tp_count)]
    gate_full = jnp.concatenate([w_gate[0], lax.ppermute(w_gate[0], "tp", swap)], 1)
    up_full = jnp.concatenate([w_up[0], lax.ppermute(w_up[0], "tp", swap)], 1)
    down_full = jnp.concatenate([w_down[0], lax.ppermute(w_down[0], "tp", swap)], 0)

    pieces = prefix_kv.reshape(seq_count, -1)
    piece = pieces.shape[1]
    tag = jnp.zeros((seq_count, 128), pieces.dtype).at[:, :depth].set(
        jnp.broadcast_to(path.astype(pieces.dtype), (seq_count, depth))
    )
    spread = lax.all_to_all(jnp.concatenate([pieces, tag], 1), "seq", 0, 0, tiled=True)
    paths = spread[:, piece : piece + depth].astype(jnp.int32)
    spread = spread[:, :piece]
    node_ids = jnp.arange(spread.shape[0], dtype=jnp.int32)
    pick = (paths.reshape(-1)[:, None] == node_ids[None, :]).astype(spread.dtype)
    picked = jnp.dot(pick, spread, preferred_element_type=jnp.float32).astype(spread.dtype)
    got = lax.all_to_all(picked.reshape(seq_count, depth * piece), "seq", 0, 0, tiled=True)
    nodes_kv = got.reshape(seq_count, depth, piece).transpose(1, 0, 2).reshape(depth, 2, slot, width)
    prefix_keys = nodes_kv[:, 0].reshape(depth * slot, heads_here, HD)
    prefix_values = nodes_kv[:, 1].reshape(depth * slot, heads_here, HD)

    my_nodes = path[0]
    lengths = jnp.sum(
        jnp.where(my_nodes[:, None] == node_ids[None, :], node_len[None, :], 0), axis=1
    )
    live = (jnp.arange(slot, dtype=jnp.int32)[None, :] < lengths[:, None]).reshape(-1)
    live_all = jnp.concatenate([jnp.ones((rows,), dtype=bool), live])

    queries = query.reshape(rows, heads_here, HD)
    keys = jnp.concatenate([suffix_kv[0].reshape(rows, heads_here, HD), prefix_keys], 0)
    values = jnp.concatenate(
        [suffix_kv[1].reshape(rows, heads_here, HD), prefix_values], 0
    ).astype(jnp.float32)
    scores = (
        jnp.einsum("qhd,khd->hqk", queries, keys, preferred_element_type=jnp.float32) * scale
    )
    scores = jnp.where(live_all[None, None, :], scores, -jnp.inf)
    top = jnp.max(scores, axis=2)
    probs = jnp.exp(scores - top[:, :, None])
    total = jnp.sum(probs, axis=2)
    accum = jnp.einsum("hqk,khd->hqd", probs, values)
    attn = (accum / total[:, :, None]).astype(jnp.bfloat16)
    partial_value = jnp.einsum(
        "hqd,hdm->qm",
        attn,
        out_weight.reshape(heads_here, HD, D),
        preferred_element_type=jnp.float32,
    )
    heads_sum = partial_value + lax.ppermute(partial_value, "tp", swap)
    hidden_state = layer_input.astype(jnp.float32) + heads_sum
    mean_square = jnp.mean(hidden_state * hidden_state, axis=1, keepdims=True)
    normed = (hidden_state * lax.rsqrt(mean_square + 1e-06) * norm_gain).astype(jnp.bfloat16)

    experts = w_gate.shape[0] * seq_count
    cap = 5 * rows * TOPK // (4 * experts)
    share = -(-(-(-cap // tp_count)) // 8) * 8
    hit = expert_ids[:, :, None] == jnp.arange(experts, dtype=jnp.int32)[None, None, :]
    chosen = jnp.any(hit, axis=1)
    weight_of = jnp.sum(jnp.where(hit, gates[:, :, None], 0.0), axis=1)
    token = jnp.arange(rows, dtype=jnp.int32)
    earlier = (token[None, :] < token[:, None]).astype(jnp.bfloat16)
    ranks = jnp.dot(
        earlier, chosen.astype(jnp.bfloat16), preferred_element_type=jnp.float32
    ).astype(jnp.int32)
    target = tp_count * jnp.arange(share, dtype=jnp.int32) + tp_index
    sel = chosen[:, :, None] & (ranks[:, :, None] == target[None, None, :])
    sel = sel.reshape(rows, experts * share).astype(jnp.bfloat16)
    outgoing = jnp.einsum(
        "ts,td->sd", sel, normed, preferred_element_type=jnp.float32
    ).astype(jnp.bfloat16)
    arrived = lax.all_to_all(
        outgoing.reshape(experts, share, D), "seq", 0, 0, tiled=True
    ).reshape(experts * share, D)
    gate_part = jnp.dot(arrived, gate_full, preferred_element_type=jnp.float32)
    up_part = jnp.dot(arrived, up_full, preferred_element_type=jnp.float32)
    act = (jax.nn.silu(gate_part) * up_part).astype(jnp.bfloat16)
    half = D // tp_count
    result = jnp.einsum(
        "sf,fuc->usc",
        act,
        down_full.reshape(down_full.shape[0], tp_count, half),
        preferred_element_type=jnp.float32,
    ).astype(jnp.bfloat16)
    back = lax.all_to_all(
        result.reshape(tp_count * experts, share, half), ("tp", "seq"), 0, 0, tiled=True
    )
    back = back.reshape(tp_count * experts * share, half)

    spot = (
        tp_count * jnp.arange(share, dtype=jnp.int32)[None, None, :]
        + jnp.arange(tp_count, dtype=jnp.int32)[:, None, None]
    )
    combine = jnp.where(
        chosen.T[None, :, :, None] & (ranks.T[None, :, :, None] == spot[:, None, :, :]),
        weight_of.T[None, :, :, None],
        0.0,
    )
    combine = jnp.moveaxis(combine, 2, 0).reshape(rows, -1)
    combine_hi = combine.astype(jnp.bfloat16)
    combine_lo = (combine - combine_hi.astype(jnp.float32)).astype(jnp.bfloat16)
    both = lax.optimization_barrier(jnp.concatenate([combine_hi, combine_lo], 0))
    parts = jnp.dot(both, back, preferred_element_type=jnp.float32)
    mixture = parts[:rows] + parts[rows:]
    residual = lax.dynamic_slice_in_dim(hidden_state, tp_index * half, half, 1)
    return (residual + mixture).astype(jnp.bfloat16)


def solution(mesh):
    in_specs = (
        P("seq", None),
        P("seq", "tp"),
        P(None, "seq", "tp"),
        P(None, "seq", "tp"),
        P(),
        P("seq", None),
        P("tp", None),
        P(),
        P("seq", None),
        P("seq", None),
        P("seq", None, "tp"),
        P("seq", None, "tp"),
        P("seq", "tp", None),
    )
    out_specs = P("seq", "tp")
    return jax.shard_map(local, mesh=mesh, in_specs=in_specs, out_specs=out_specs, check_vma=False)
```

```python
import math

import jax
import jax.numpy as jnp
from jax import lax
from jax.sharding import PartitionSpec as P

D = 2048
HD = 128
TOPK = 8


def local(
    layer_input,
    query,
    suffix_kv,
    prefix_kv,
    node_len,
    path,
    out_weight,
    norm_gain,
    expert_ids,
    gates,
    w_gate,
    w_up,
    w_down,
):
    rows = query.shape[0]
    width = query.shape[1]
    heads_here = width // HD
    scale = 1.0 / math.sqrt(HD)
    seq_count = lax.axis_size("seq")
    tp_index = lax.axis_index("tp")
    tp_count = lax.axis_size("tp")
    depth = path.shape[1]
    slot = prefix_kv.shape[1]

    swap = [(i, (i + 1) % tp_count) for i in range(tp_count)]
    gate_full = jnp.concatenate([w_gate[0], lax.ppermute(w_gate[0], "tp", swap)], 1)
    up_full = jnp.concatenate([w_up[0], lax.ppermute(w_up[0], "tp", swap)], 1)
    down_full = jnp.concatenate([w_down[0], lax.ppermute(w_down[0], "tp", swap)], 0)

    pieces = prefix_kv.reshape(seq_count, -1)
    piece = pieces.shape[1]
    tag = jnp.zeros((seq_count, 128), pieces.dtype).at[:, :depth].set(
        jnp.broadcast_to(path.astype(pieces.dtype), (seq_count, depth))
    )
    spread = lax.all_to_all(jnp.concatenate([pieces, tag], 1), "seq", 0, 0, tiled=True)
    paths = spread[:, piece : piece + depth].astype(jnp.int32)
    spread = spread[:, :piece]
    node_ids = jnp.arange(spread.shape[0], dtype=jnp.int32)
    pick = (paths.reshape(-1)[:, None] == node_ids[None, :]).astype(spread.dtype)
    picked = jnp.dot(pick, spread, preferred_element_type=jnp.float32).astype(spread.dtype)
    got = lax.all_to_all(picked.reshape(seq_count, depth * piece), "seq", 0, 0, tiled=True)
    nodes_kv = got.reshape(seq_count, depth, piece).transpose(1, 0, 2).reshape(depth, 2, slot, width)
    prefix_keys = nodes_kv[:, 0].reshape(depth * slot, heads_here, HD)
    prefix_values = nodes_kv[:, 1].reshape(depth * slot, heads_here, HD)

    my_nodes = path[0]
    lengths = jnp.sum(
        jnp.where(my_nodes[:, None] == node_ids[None, :], node_len[None, :], 0), axis=1
    )
    live = (jnp.arange(slot, dtype=jnp.int32)[None, :] < lengths[:, None]).reshape(-1)
    live_all = jnp.concatenate([jnp.ones((rows,), dtype=bool), live])

    queries = query.reshape(rows, heads_here, HD)
    keys = jnp.concatenate([suffix_kv[0].reshape(rows, heads_here, HD), prefix_keys], 0)
    values = jnp.concatenate(
        [suffix_kv[1].reshape(rows, heads_here, HD), prefix_values], 0
    ).astype(jnp.float32)
    scores = (
        jnp.einsum("qhd,khd->hqk", queries, keys, preferred_element_type=jnp.float32) * scale
    )
    scores = jnp.where(live_all[None, None, :], scores, -jnp.inf)
    top = jnp.max(scores, axis=2)
    probs = jnp.exp(scores - top[:, :, None])
    total = jnp.sum(probs, axis=2)
    accum = jnp.einsum("hqk,khd->hqd", probs, values)
    attn = (accum / total[:, :, None]).astype(jnp.bfloat16)
    partial_value = jnp.einsum(
        "hqd,hdm->qm",
        attn,
        out_weight.reshape(heads_here, HD, D),
        preferred_element_type=jnp.float32,
    )
    heads_sum = partial_value + lax.ppermute(partial_value, "tp", swap)
    hidden_state = layer_input.astype(jnp.float32) + heads_sum
    mean_square = jnp.mean(hidden_state * hidden_state, axis=1, keepdims=True)
    normed = (hidden_state * lax.rsqrt(mean_square + 1e-06) * norm_gain).astype(jnp.bfloat16)

    experts = w_gate.shape[0] * seq_count
    cap = 5 * rows * TOPK // (4 * experts)
    share = -(-(-(-cap // tp_count)) // 8) * 8
    hit = expert_ids[:, :, None] == jnp.arange(experts, dtype=jnp.int32)[None, None, :]
    chosen = jnp.any(hit, axis=1)
    weight_of = jnp.sum(jnp.where(hit, gates[:, :, None], 0.0), axis=1)
    token = jnp.arange(rows, dtype=jnp.int32)
    earlier = (token[None, :] < token[:, None]).astype(jnp.bfloat16)
    ranks = jnp.dot(
        earlier, chosen.astype(jnp.bfloat16), preferred_element_type=jnp.float32
    ).astype(jnp.int32)
    target = tp_count * jnp.arange(share, dtype=jnp.int32) + tp_index
    sel = chosen[:, :, None] & (ranks[:, :, None] == target[None, None, :])
    sel = sel.reshape(rows, experts * share).astype(jnp.bfloat16)
    outgoing = jnp.einsum(
        "ts,td->sd", sel, normed, preferred_element_type=jnp.float32
    ).astype(jnp.bfloat16)
    arrived = lax.all_to_all(
        outgoing.reshape(experts, share, D), "seq", 0, 0, tiled=True
    ).reshape(experts * share, D)
    gate_part = jnp.dot(arrived, gate_full, preferred_element_type=jnp.float32)
    up_part = jnp.dot(arrived, up_full, preferred_element_type=jnp.float32)
    act = (jax.nn.silu(gate_part) * up_part).astype(jnp.bfloat16)
    half = D // tp_count
    down_cols = down_full.reshape(down_full.shape[0], tp_count, half)
    result = jnp.stack(
        [
            jnp.dot(act, down_cols[:, u], preferred_element_type=jnp.float32).astype(jnp.bfloat16)
            for u in range(tp_count)
        ]
    )
    back = lax.all_to_all(
        result.reshape(tp_count * experts, share, half), ("tp", "seq"), 0, 0, tiled=True
    )
    back = back.reshape(tp_count * experts * share, half)

    spot = (
        tp_count * jnp.arange(share, dtype=jnp.int32)[None, None, :]
        + jnp.arange(tp_count, dtype=jnp.int32)[:, None, None]
    )
    combine = jnp.where(
        chosen.T[None, :, :, None] & (ranks.T[None, :, :, None] == spot[:, None, :, :]),
        weight_of.T[None, :, :, None],
        0.0,
    )
    combine = jnp.moveaxis(combine, 2, 0).reshape(rows, -1)
    combine_hi = combine.astype(jnp.bfloat16)
    combine_lo = (combine - combine_hi.astype(jnp.float32)).astype(jnp.bfloat16)
    both = lax.optimization_barrier(jnp.concatenate([combine_hi, combine_lo], 0))
    parts = jnp.dot(both, back, preferred_element_type=jnp.float32)
    mixture = parts[:rows] + parts[rows:]
    residual = lax.dynamic_slice_in_dim(hidden_state, tp_index * half, half, 1)
    return (residual + mixture).astype(jnp.bfloat16)


def solution(mesh):
    in_specs = (
        P("seq", None),
        P("seq", "tp"),
        P(None, "seq", "tp"),
        P(None, "seq", "tp"),
        P(),
        P("seq", None),
        P("tp", None),
        P(),
        P("seq", None),
        P("seq", None),
        P("seq", None, "tp"),
        P("seq", None, "tp"),
        P("seq", "tp", None),
    )
    out_specs = P("seq", "tp")
    return jax.shard_map(local, mesh=mesh, in_specs=in_specs, out_specs=out_specs, check_vma=False)
```

```python
import math

import jax
import jax.numpy as jnp
from jax import lax
from jax.sharding import PartitionSpec as P

D = 2048
HD = 128
TOPK = 8


def local(
    layer_input,
    query,
    suffix_kv,
    prefix_kv,
    node_len,
    path,
    out_weight,
    norm_gain,
    expert_ids,
    gates,
    w_gate,
    w_up,
    w_down,
):
    rows = query.shape[0]
    width = query.shape[1]
    heads_here = width // HD
    scale = 1.0 / math.sqrt(HD)
    seq_count = lax.axis_size("seq")
    tp_index = lax.axis_index("tp")
    tp_count = lax.axis_size("tp")
    depth = path.shape[1]
    slot = prefix_kv.shape[1]

    swap = [(i, (i + 1) % tp_count) for i in range(tp_count)]
    gate_full = jnp.concatenate([w_gate[0], lax.ppermute(w_gate[0], "tp", swap)], 1)
    up_full = jnp.concatenate([w_up[0], lax.ppermute(w_up[0], "tp", swap)], 1)
    down_full = jnp.concatenate([w_down[0], lax.ppermute(w_down[0], "tp", swap)], 0)

    pieces = prefix_kv.reshape(seq_count, -1)
    piece = pieces.shape[1]
    tag = jnp.zeros((seq_count, 128), pieces.dtype).at[:, :depth].set(
        jnp.broadcast_to(path.astype(pieces.dtype), (seq_count, depth))
    )
    spread = lax.all_to_all(jnp.concatenate([pieces, tag], 1), "seq", 0, 0, tiled=True)
    paths = spread[:, piece : piece + depth].astype(jnp.int32)
    spread = spread[:, :piece]
    node_ids = jnp.arange(spread.shape[0], dtype=jnp.int32)
    pick = (paths.reshape(-1)[:, None] == node_ids[None, :]).astype(spread.dtype)
    picked = jnp.dot(pick, spread, preferred_element_type=jnp.float32).astype(spread.dtype)
    got = lax.all_to_all(picked.reshape(seq_count, depth * piece), "seq", 0, 0, tiled=True)
    nodes_kv = got.reshape(seq_count, depth, piece).transpose(1, 0, 2).reshape(depth, 2, slot, width)
    prefix_keys = nodes_kv[:, 0].reshape(depth * slot, heads_here, HD)
    prefix_values = nodes_kv[:, 1].reshape(depth * slot, heads_here, HD)

    my_nodes = path[0]
    lengths = jnp.sum(
        jnp.where(my_nodes[:, None] == node_ids[None, :], node_len[None, :], 0), axis=1
    )
    live = (jnp.arange(slot, dtype=jnp.int32)[None, :] < lengths[:, None]).reshape(-1)
    live_all = jnp.concatenate([jnp.ones((rows,), dtype=bool), live])

    queries = query.reshape(rows, heads_here, HD)
    keys = jnp.concatenate([suffix_kv[0].reshape(rows, heads_here, HD), prefix_keys], 0)
    values = jnp.concatenate(
        [suffix_kv[1].reshape(rows, heads_here, HD), prefix_values], 0
    ).astype(jnp.float32)
    scores = (
        jnp.einsum("qhd,khd->hqk", queries, keys, preferred_element_type=jnp.float32) * scale
    )
    scores = jnp.where(live_all[None, None, :], scores, -jnp.inf)
    top = jnp.max(scores, axis=2)
    probs = jnp.exp(scores - top[:, :, None])
    total = jnp.sum(probs, axis=2)
    accum = jnp.einsum("hqk,khd->hqd", probs, values)
    attn = (accum / total[:, :, None]).astype(jnp.bfloat16)
    partial_value = jnp.einsum(
        "hqd,hdm->qm",
        attn,
        out_weight.reshape(heads_here, HD, D),
        preferred_element_type=jnp.float32,
    )
    heads_sum = partial_value + lax.ppermute(partial_value, "tp", swap)
    hidden_state = layer_input.astype(jnp.float32) + heads_sum
    mean_square = jnp.mean(hidden_state * hidden_state, axis=1, keepdims=True)
    normed = (hidden_state * lax.rsqrt(mean_square + 1e-06) * norm_gain).astype(jnp.bfloat16)

    experts = w_gate.shape[0] * seq_count
    cap = 5 * rows * TOPK // (4 * experts)
    share = -(-(-(-cap // tp_count)) // 8) * 8
    hit = expert_ids[:, :, None] == jnp.arange(experts, dtype=jnp.int32)[None, None, :]
    chosen = jnp.any(hit, axis=1)
    weight_of = jnp.sum(jnp.where(hit, gates[:, :, None], 0.0), axis=1)
    token = jnp.arange(rows, dtype=jnp.int32)
    earlier = (token[None, :] < token[:, None]).astype(jnp.bfloat16)
    ranks = jnp.dot(
        earlier, chosen.astype(jnp.bfloat16), preferred_element_type=jnp.float32
    ).astype(jnp.int32)
    half = D // tp_count
    down_cols = down_full.reshape(down_full.shape[0], tp_count, half)
    first = max(8, share // 16 * 8)
    mixture = None
    for lo, hi in ((0, first), (first, share)):
        count = hi - lo
        target = tp_count * jnp.arange(lo, hi, dtype=jnp.int32) + tp_index
        sel = chosen[:, :, None] & (ranks[:, :, None] == target[None, None, :])
        sel = sel.reshape(rows, experts * count).astype(jnp.bfloat16)
        outgoing = jnp.einsum(
            "ts,td->sd", sel, normed, preferred_element_type=jnp.float32
        ).astype(jnp.bfloat16)
        arrived = lax.all_to_all(
            outgoing.reshape(experts, count, D), "seq", 0, 0, tiled=True
        ).reshape(experts * count, D)
        gate_part = jnp.dot(arrived, gate_full, preferred_element_type=jnp.float32)
        up_part = jnp.dot(arrived, up_full, preferred_element_type=jnp.float32)
        act = (jax.nn.silu(gate_part) * up_part).astype(jnp.bfloat16)
        result = jnp.stack(
            [
                jnp.dot(act, down_cols[:, u], preferred_element_type=jnp.float32).astype(
                    jnp.bfloat16
                )
                for u in range(tp_count)
            ]
        )
        back = lax.all_to_all(
            result.reshape(tp_count * experts, count, half), ("tp", "seq"), 0, 0, tiled=True
        )
        back = back.reshape(tp_count * experts * count, half)

        spot = (
            tp_count * jnp.arange(lo, hi, dtype=jnp.int32)[None, None, :]
            + jnp.arange(tp_count, dtype=jnp.int32)[:, None, None]
        )
        combine = jnp.where(
            chosen.T[None, :, :, None] & (ranks.T[None, :, :, None] == spot[:, None, :, :]),
            weight_of.T[None, :, :, None],
            0.0,
        )
        combine = jnp.moveaxis(combine, 2, 0).reshape(rows, -1)
        combine_hi = combine.astype(jnp.bfloat16)
        combine_lo = (combine - combine_hi.astype(jnp.float32)).astype(jnp.bfloat16)
        both = lax.optimization_barrier(jnp.concatenate([combine_hi, combine_lo], 0))
        parts = jnp.dot(both, back, preferred_element_type=jnp.float32)
        piece_sum = parts[:rows] + parts[rows:]
        mixture = piece_sum if mixture is None else mixture + piece_sum
    residual = lax.dynamic_slice_in_dim(hidden_state, tp_index * half, half, 1)
    return (residual + mixture).astype(jnp.bfloat16)


def solution(mesh):
    in_specs = (
        P("seq", None),
        P("seq", "tp"),
        P(None, "seq", "tp"),
        P(None, "seq", "tp"),
        P(),
        P("seq", None),
        P("tp", None),
        P(),
        P("seq", None),
        P("seq", None),
        P("seq", None, "tp"),
        P("seq", None, "tp"),
        P("seq", "tp", None),
    )
    out_specs = P("seq", "tp")
    return jax.shard_map(local, mesh=mesh, in_specs=in_specs, out_specs=out_specs, check_vma=False)
```

```python
import math

import jax
import jax.numpy as jnp
from jax import lax
from jax.sharding import PartitionSpec as P

D = 2048
HD = 128
TOPK = 8


def local(
    layer_input,
    query,
    suffix_kv,
    prefix_kv,
    node_len,
    path,
    out_weight,
    norm_gain,
    expert_ids,
    gates,
    w_gate,
    w_up,
    w_down,
):
    rows = query.shape[0]
    width = query.shape[1]
    heads_here = width // HD
    scale = 1.0 / math.sqrt(HD)
    seq_count = lax.axis_size("seq")
    tp_index = lax.axis_index("tp")
    tp_count = lax.axis_size("tp")
    depth = path.shape[1]
    slot = prefix_kv.shape[1]

    swap = [(i, (i + 1) % tp_count) for i in range(tp_count)]
    gate_full = jnp.concatenate([w_gate[0], lax.ppermute(w_gate[0], "tp", swap)], 1)
    up_full = jnp.concatenate([w_up[0], lax.ppermute(w_up[0], "tp", swap)], 1)
    down_full = jnp.concatenate([w_down[0], lax.ppermute(w_down[0], "tp", swap)], 0)

    pieces = prefix_kv.reshape(seq_count, -1)
    piece = pieces.shape[1]
    tag = jnp.zeros((seq_count, 128), pieces.dtype).at[:, :depth].set(
        jnp.broadcast_to(path.astype(pieces.dtype), (seq_count, depth))
    )
    spread = lax.all_to_all(jnp.concatenate([pieces, tag], 1), "seq", 0, 0, tiled=True)
    paths = spread[:, piece : piece + depth].astype(jnp.int32)
    spread = spread[:, :piece]
    node_ids = jnp.arange(spread.shape[0], dtype=jnp.int32)
    pick = (paths.reshape(-1)[:, None] == node_ids[None, :]).astype(spread.dtype)
    picked = jnp.dot(pick, spread, preferred_element_type=jnp.float32).astype(spread.dtype)
    got = lax.all_to_all(picked.reshape(seq_count, depth * piece), "seq", 0, 0, tiled=True)
    nodes_kv = got.reshape(seq_count, depth, piece).transpose(1, 0, 2).reshape(depth, 2, slot, width)
    prefix_keys = nodes_kv[:, 0].reshape(depth * slot, heads_here, HD)
    prefix_values = nodes_kv[:, 1].reshape(depth * slot, heads_here, HD)

    my_nodes = path[0]
    lengths = jnp.sum(
        jnp.where(my_nodes[:, None] == node_ids[None, :], node_len[None, :], 0), axis=1
    )
    live = (jnp.arange(slot, dtype=jnp.int32)[None, :] < lengths[:, None]).reshape(-1)
    live_all = jnp.concatenate([jnp.ones((rows,), dtype=bool), live])

    queries = query.reshape(rows, heads_here, HD)
    keys = jnp.concatenate([suffix_kv[0].reshape(rows, heads_here, HD), prefix_keys], 0)
    values = jnp.concatenate(
        [suffix_kv[1].reshape(rows, heads_here, HD), prefix_values], 0
    ).astype(jnp.float32)
    scores = (
        jnp.einsum("qhd,khd->hqk", queries, keys, preferred_element_type=jnp.float32) * scale
    )
    scores = jnp.where(live_all[None, None, :], scores, -jnp.inf)
    top = jnp.max(scores, axis=2)
    probs = jnp.exp(scores - top[:, :, None])
    total = jnp.sum(probs, axis=2)
    accum = jnp.einsum("hqk,khd->hqd", probs, values)
    attn = (accum / total[:, :, None]).astype(jnp.bfloat16)
    partial_value = jnp.einsum(
        "hqd,hdm->qm",
        attn,
        out_weight.reshape(heads_here, HD, D),
        preferred_element_type=jnp.float32,
    )
    heads_sum = partial_value + lax.ppermute(partial_value, "tp", swap)
    hidden_state = layer_input.astype(jnp.float32) + heads_sum
    mean_square = jnp.mean(hidden_state * hidden_state, axis=1, keepdims=True)
    normed = (hidden_state * lax.rsqrt(mean_square + 1e-06) * norm_gain).astype(jnp.bfloat16)

    experts = w_gate.shape[0] * seq_count
    cap = 5 * rows * TOPK // (4 * experts)
    share = -(-(-(-cap // tp_count)) // 8) * 8
    hit = expert_ids[:, :, None] == jnp.arange(experts, dtype=jnp.int32)[None, None, :]
    chosen = jnp.any(hit, axis=1)
    weight_of = jnp.sum(jnp.where(hit, gates[:, :, None], 0.0), axis=1)
    token = jnp.arange(rows, dtype=jnp.int32)
    earlier = (token[None, :] < token[:, None]).astype(jnp.bfloat16)
    ranks = jnp.dot(
        earlier, chosen.astype(jnp.bfloat16), preferred_element_type=jnp.float32
    ).astype(jnp.int32)
    half = D // tp_count
    down_cols = down_full.reshape(down_full.shape[0], tp_count, half)
    first = cap // tp_count // 8 * 8
    main = tp_count * first
    over = -(-(cap - main) // 8) * 8

    def combine_with(back, spot):
        combine = jnp.where(
            chosen.T[None, :, :, None] & (ranks.T[None, :, :, None] == spot[:, None, None, :]),
            weight_of.T[None, :, :, None],
            0.0,
        )
        combine = jnp.moveaxis(combine, 2, 0).reshape(rows, -1)
        combine_hi = combine.astype(jnp.bfloat16)
        combine_lo = (combine - combine_hi.astype(jnp.float32)).astype(jnp.bfloat16)
        both = lax.optimization_barrier(jnp.concatenate([combine_hi, combine_lo], 0))
        parts = jnp.dot(both, back, preferred_element_type=jnp.float32)
        return parts[:rows] + parts[rows:]

    def expert_rows(arrived):
        gate_part = jnp.dot(arrived, gate_full, preferred_element_type=jnp.float32)
        up_part = jnp.dot(arrived, up_full, preferred_element_type=jnp.float32)
        return (jax.nn.silu(gate_part) * up_part).astype(jnp.bfloat16)

    def select(wanted):
        sel = chosen[:, :, None] & (ranks[:, :, None] == wanted[None, None, :])
        return sel.reshape(rows, experts * wanted.shape[0]).astype(jnp.bfloat16)

    mine = lax.dynamic_slice_in_dim(normed, tp_index * half, half, 1)
    extra = jnp.arange(main, main + over, dtype=jnp.int32)
    outgoing = jnp.einsum(
        "ts,td->sd", select(extra), mine, preferred_element_type=jnp.float32
    ).astype(jnp.bfloat16)
    arrived = lax.all_to_all(outgoing.reshape(experts, over, half), "seq", 0, 0, tiled=True)
    arrived = arrived.reshape(experts * over, half)
    partner = lax.ppermute(arrived, "tp", swap)
    arrived = jnp.where(
        tp_index == 0,
        jnp.concatenate([arrived, partner], 1),
        jnp.concatenate([partner, arrived], 1),
    )
    act = expert_rows(arrived)
    result = jnp.dot(
        act, lax.dynamic_slice_in_dim(down_cols, tp_index, 1, 1)[:, 0],
        preferred_element_type=jnp.float32,
    ).astype(jnp.bfloat16)
    back = lax.all_to_all(result.reshape(experts, over, half), "seq", 0, 0, tiled=True)
    mixture = combine_with(back.reshape(experts * over, half), extra[None, :])

    target = tp_count * jnp.arange(first, dtype=jnp.int32) + tp_index
    outgoing = jnp.einsum(
        "ts,td->sd", select(target), normed, preferred_element_type=jnp.float32
    ).astype(jnp.bfloat16)
    arrived = lax.all_to_all(
        outgoing.reshape(experts, first, D), "seq", 0, 0, tiled=True
    ).reshape(experts * first, D)
    act = expert_rows(arrived)
    result = jnp.stack(
        [
            jnp.dot(act, down_cols[:, u], preferred_element_type=jnp.float32).astype(jnp.bfloat16)
            for u in range(tp_count)
        ]
    )
    back = lax.all_to_all(
        result.reshape(tp_count * experts, first, half), ("tp", "seq"), 0, 0, tiled=True
    )
    spot = (
        tp_count * jnp.arange(first, dtype=jnp.int32)[None, :]
        + jnp.arange(tp_count, dtype=jnp.int32)[:, None]
    )
    mixture = mixture + combine_with(back.reshape(-1, half), spot)
    residual = lax.dynamic_slice_in_dim(hidden_state, tp_index * half, half, 1)
    return (residual + mixture).astype(jnp.bfloat16)


def solution(mesh):
    in_specs = (
        P("seq", None),
        P("seq", "tp"),
        P(None, "seq", "tp"),
        P(None, "seq", "tp"),
        P(),
        P("seq", None),
        P("tp", None),
        P(),
        P("seq", None),
        P("seq", None),
        P("seq", None, "tp"),
        P("seq", None, "tp"),
        P("seq", "tp", None),
    )
    out_specs = P("seq", "tp")
    return jax.shard_map(local, mesh=mesh, in_specs=in_specs, out_specs=out_specs, check_vma=False)
```

```python
import math

import jax
import jax.numpy as jnp
from jax import lax
from jax.sharding import PartitionSpec as P

D = 2048
HD = 128
TOPK = 8


def local(
    layer_input,
    query,
    suffix_kv,
    prefix_kv,
    node_len,
    path,
    out_weight,
    norm_gain,
    expert_ids,
    gates,
    w_gate,
    w_up,
    w_down,
):
    rows = query.shape[0]
    width = query.shape[1]
    heads_here = width // HD
    scale = 1.0 / math.sqrt(HD)
    seq_count = lax.axis_size("seq")
    tp_index = lax.axis_index("tp")
    tp_count = lax.axis_size("tp")
    depth = path.shape[1]
    slot = prefix_kv.shape[1]

    swap = [(i, (i + 1) % tp_count) for i in range(tp_count)]
    gate_full = jnp.concatenate([w_gate[0], lax.ppermute(w_gate[0], "tp", swap)], 1)
    up_full = jnp.concatenate([w_up[0], lax.ppermute(w_up[0], "tp", swap)], 1)
    down_full = jnp.concatenate([w_down[0], lax.ppermute(w_down[0], "tp", swap)], 0)

    pieces = prefix_kv.reshape(seq_count, -1)
    piece = pieces.shape[1]
    tag = jnp.zeros((seq_count, 128), pieces.dtype).at[:, :depth].set(
        jnp.broadcast_to(path.astype(pieces.dtype), (seq_count, depth))
    )
    outbound = jnp.concatenate([pieces, tag], 1)
    spread = lax.all_to_all(
        outbound.reshape(seq_count, -1, 128), "seq", 0, 0, tiled=True
    ).reshape(seq_count, -1)
    paths = spread[:, piece : piece + depth].astype(jnp.int32)
    spread = spread[:, :piece]
    node_ids = jnp.arange(spread.shape[0], dtype=jnp.int32)
    pick = (paths.reshape(-1)[:, None] == node_ids[None, :]).astype(spread.dtype)
    picked = jnp.dot(pick, spread, preferred_element_type=jnp.float32).astype(spread.dtype)
    got = lax.all_to_all(
        picked.reshape(seq_count, depth * piece // 128, 128), "seq", 0, 0, tiled=True
    )
    nodes_kv = got.reshape(seq_count, depth, piece).transpose(1, 0, 2).reshape(depth, 2, slot, width)
    prefix_keys = nodes_kv[:, 0].reshape(depth * slot, heads_here, HD)
    prefix_values = nodes_kv[:, 1].reshape(depth * slot, heads_here, HD)

    my_nodes = path[0]
    lengths = jnp.sum(
        jnp.where(my_nodes[:, None] == node_ids[None, :], node_len[None, :], 0), axis=1
    )
    live = (jnp.arange(slot, dtype=jnp.int32)[None, :] < lengths[:, None]).reshape(-1)
    live_all = jnp.concatenate([jnp.ones((rows,), dtype=bool), live])

    queries = query.reshape(rows, heads_here, HD)
    keys = jnp.concatenate([suffix_kv[0].reshape(rows, heads_here, HD), prefix_keys], 0)
    values = jnp.concatenate(
        [suffix_kv[1].reshape(rows, heads_here, HD), prefix_values], 0
    ).astype(jnp.float32)
    scores = (
        jnp.einsum("qhd,khd->hqk", queries, keys, preferred_element_type=jnp.float32) * scale
    )
    scores = jnp.where(live_all[None, None, :], scores, -jnp.inf)
    top = jnp.max(scores, axis=2)
    probs = jnp.exp(scores - top[:, :, None])
    total = jnp.sum(probs, axis=2)
    accum = jnp.einsum("hqk,khd->hqd", probs, values)
    attn = (accum / total[:, :, None]).astype(jnp.bfloat16)
    partial_value = jnp.einsum(
        "hqd,hdm->qm",
        attn,
        out_weight.reshape(heads_here, HD, D),
        preferred_element_type=jnp.float32,
    )
    heads_sum = partial_value + lax.ppermute(partial_value, "tp", swap)
    hidden_state = layer_input.astype(jnp.float32) + heads_sum
    mean_square = jnp.mean(hidden_state * hidden_state, axis=1, keepdims=True)
    normed = (hidden_state * lax.rsqrt(mean_square + 1e-06) * norm_gain).astype(jnp.bfloat16)

    experts = w_gate.shape[0] * seq_count
    cap = 5 * rows * TOPK // (4 * experts)
    share = -(-(-(-cap // tp_count)) // 8) * 8
    hit = expert_ids[:, :, None] == jnp.arange(experts, dtype=jnp.int32)[None, None, :]
    chosen = jnp.any(hit, axis=1)
    weight_of = jnp.sum(jnp.where(hit, gates[:, :, None], 0.0), axis=1)
    token = jnp.arange(rows, dtype=jnp.int32)
    earlier = (token[None, :] < token[:, None]).astype(jnp.bfloat16)
    ranks = jnp.dot(
        earlier, chosen.astype(jnp.bfloat16), preferred_element_type=jnp.float32
    ).astype(jnp.int32)
    half = D // tp_count
    down_cols = down_full.reshape(down_full.shape[0], tp_count, half)
    first = cap // tp_count // 8 * 8
    main = tp_count * first
    over = -(-(cap - main) // 8) * 8

    def combine_with(back, spot):
        combine = jnp.where(
            chosen.T[None, :, :, None] & (ranks.T[None, :, :, None] == spot[:, None, None, :]),
            weight_of.T[None, :, :, None],
            0.0,
        )
        combine = jnp.moveaxis(combine, 2, 0).reshape(rows, -1)
        combine_hi = combine.astype(jnp.bfloat16)
        combine_lo = (combine - combine_hi.astype(jnp.float32)).astype(jnp.bfloat16)
        both = lax.optimization_barrier(jnp.concatenate([combine_hi, combine_lo], 0))
        parts = jnp.dot(both, back, preferred_element_type=jnp.float32)
        return parts[:rows] + parts[rows:]

    def expert_rows(arrived):
        gate_part = jnp.dot(arrived, gate_full, preferred_element_type=jnp.float32)
        up_part = jnp.dot(arrived, up_full, preferred_element_type=jnp.float32)
        return (jax.nn.silu(gate_part) * up_part).astype(jnp.bfloat16)

    def select(wanted):
        sel = chosen[:, :, None] & (ranks[:, :, None] == wanted[None, None, :])
        return sel.reshape(rows, experts * wanted.shape[0]).astype(jnp.bfloat16)

    mine = lax.dynamic_slice_in_dim(normed, tp_index * half, half, 1)
    extra = jnp.arange(main, main + over, dtype=jnp.int32)
    outgoing = jnp.einsum(
        "ts,td->sd", select(extra), mine, preferred_element_type=jnp.float32
    ).astype(jnp.bfloat16)
    arrived = lax.all_to_all(outgoing.reshape(experts, over, half), "seq", 0, 0, tiled=True)
    arrived = arrived.reshape(experts * over, half)
    partner = lax.ppermute(arrived, "tp", swap)
    arrived = jnp.where(
        tp_index == 0,
        jnp.concatenate([arrived, partner], 1),
        jnp.concatenate([partner, arrived], 1),
    )
    act = expert_rows(arrived)
    result = jnp.dot(
        act, lax.dynamic_slice_in_dim(down_cols, tp_index, 1, 1)[:, 0],
        preferred_element_type=jnp.float32,
    ).astype(jnp.bfloat16)
    back = lax.all_to_all(result.reshape(experts, over, half), "seq", 0, 0, tiled=True)
    mixture = combine_with(back.reshape(experts * over, half), extra[None, :])

    target = tp_count * jnp.arange(first, dtype=jnp.int32) + tp_index
    outgoing = jnp.einsum(
        "ts,td->sd", select(target), normed, preferred_element_type=jnp.float32
    ).astype(jnp.bfloat16)
    arrived = lax.all_to_all(
        outgoing.reshape(experts, first, D), "seq", 0, 0, tiled=True
    ).reshape(experts * first, D)
    act = expert_rows(arrived)
    result = jnp.stack(
        [
            jnp.dot(act, down_cols[:, u], preferred_element_type=jnp.float32).astype(jnp.bfloat16)
            for u in range(tp_count)
        ]
    )
    back = lax.all_to_all(
        result.reshape(tp_count * experts, first, half), ("tp", "seq"), 0, 0, tiled=True
    )
    spot = (
        tp_count * jnp.arange(first, dtype=jnp.int32)[None, :]
        + jnp.arange(tp_count, dtype=jnp.int32)[:, None]
    )
    mixture = mixture + combine_with(back.reshape(-1, half), spot)
    residual = lax.dynamic_slice_in_dim(hidden_state, tp_index * half, half, 1)
    return (residual + mixture).astype(jnp.bfloat16)


def solution(mesh):
    in_specs = (
        P("seq", None),
        P("seq", "tp"),
        P(None, "seq", "tp"),
        P(None, "seq", "tp"),
        P(),
        P("seq", None),
        P("tp", None),
        P(),
        P("seq", None),
        P("seq", None),
        P("seq", None, "tp"),
        P("seq", None, "tp"),
        P("seq", "tp", None),
    )
    out_specs = P("seq", "tp")
    return jax.shard_map(local, mesh=mesh, in_specs=in_specs, out_specs=out_specs, check_vma=False)
```

```python
import math

import jax
import jax.numpy as jnp
from jax import lax
from jax.sharding import PartitionSpec as P

D = 2048
HD = 128
TOPK = 8


def local(
    layer_input,
    query,
    suffix_kv,
    prefix_kv,
    node_len,
    path,
    out_weight,
    norm_gain,
    expert_ids,
    gates,
    w_gate,
    w_up,
    w_down,
):
    rows = query.shape[0]
    width = query.shape[1]
    heads_here = width // HD
    scale = 1.0 / math.sqrt(HD)
    seq_count = lax.axis_size("seq")
    tp_index = lax.axis_index("tp")
    tp_count = lax.axis_size("tp")
    depth = path.shape[1]
    slot = prefix_kv.shape[1]

    swap = [(i, (i + 1) % tp_count) for i in range(tp_count)]
    gate_full = jnp.concatenate([w_gate[0], lax.ppermute(w_gate[0], "tp", swap)], 1)
    up_full = jnp.concatenate([w_up[0], lax.ppermute(w_up[0], "tp", swap)], 1)
    down_full = jnp.concatenate([w_down[0], lax.ppermute(w_down[0], "tp", swap)], 0)

    pieces = prefix_kv.reshape(seq_count, -1)
    piece = pieces.shape[1]
    tag = jnp.zeros((seq_count, 128), pieces.dtype).at[:, :depth].set(
        jnp.broadcast_to(path.astype(pieces.dtype), (seq_count, depth))
    )
    outbound = jnp.concatenate([pieces, tag], 1)
    spread = lax.all_to_all(
        outbound.reshape(seq_count, -1, 128), "seq", 0, 0, tiled=True
    ).reshape(seq_count, -1)
    paths = spread[:, piece : piece + depth].astype(jnp.int32)
    spread = spread[:, :piece]
    node_ids = jnp.arange(spread.shape[0], dtype=jnp.int32)
    pick = (paths.reshape(-1)[:, None] == node_ids[None, :]).astype(spread.dtype)
    picked = jnp.dot(pick, spread, preferred_element_type=jnp.float32).astype(spread.dtype)
    got = lax.all_to_all(
        picked.reshape(seq_count, depth * piece // 128, 128), "seq", 0, 0, tiled=True
    )
    nodes_kv = got.reshape(seq_count, depth, piece).transpose(1, 0, 2).reshape(depth, 2, slot, width)
    prefix_keys = nodes_kv[:, 0].reshape(depth * slot, heads_here, HD)
    prefix_values = nodes_kv[:, 1].reshape(depth * slot, heads_here, HD)

    my_nodes = path[0]
    lengths = jnp.sum(
        jnp.where(my_nodes[:, None] == node_ids[None, :], node_len[None, :], 0), axis=1
    )
    live = (jnp.arange(slot, dtype=jnp.int32)[None, :] < lengths[:, None]).reshape(-1)
    live_all = jnp.concatenate([jnp.ones((rows,), dtype=bool), live])

    queries = query.reshape(rows, heads_here, HD)
    keys = jnp.concatenate([suffix_kv[0].reshape(rows, heads_here, HD), prefix_keys], 0)
    values = jnp.concatenate(
        [suffix_kv[1].reshape(rows, heads_here, HD), prefix_values], 0
    ).astype(jnp.float32)
    scores = (
        jnp.einsum("qhd,khd->hqk", queries, keys, preferred_element_type=jnp.float32) * scale
    )
    scores = jnp.where(live_all[None, None, :], scores, -jnp.inf)
    top = jnp.max(scores, axis=2)
    probs = jnp.exp(scores - top[:, :, None])
    total = jnp.sum(probs, axis=2)
    accum = jnp.einsum("hqk,khd->hqd", probs, values)
    attn = lax.optimization_barrier((accum / total[:, :, None]).astype(jnp.bfloat16))
    partial_value = jnp.einsum(
        "hqd,hdm->qm",
        attn,
        out_weight.reshape(heads_here, HD, D),
        preferred_element_type=jnp.float32,
    )
    heads_sum = partial_value + lax.ppermute(partial_value, "tp", swap)
    hidden_state = layer_input.astype(jnp.float32) + heads_sum
    mean_square = jnp.mean(hidden_state * hidden_state, axis=1, keepdims=True)
    normed = (hidden_state * lax.rsqrt(mean_square + 1e-06) * norm_gain).astype(jnp.bfloat16)

    experts = w_gate.shape[0] * seq_count
    cap = 5 * rows * TOPK // (4 * experts)
    share = -(-(-(-cap // tp_count)) // 8) * 8
    hit = expert_ids[:, :, None] == jnp.arange(experts, dtype=jnp.int32)[None, None, :]
    chosen = jnp.any(hit, axis=1)
    weight_of = jnp.sum(jnp.where(hit, gates[:, :, None], 0.0), axis=1)
    token = jnp.arange(rows, dtype=jnp.int32)
    earlier = (token[None, :] < token[:, None]).astype(jnp.bfloat16)
    ranks = jnp.dot(
        earlier, chosen.astype(jnp.bfloat16), preferred_element_type=jnp.float32
    ).astype(jnp.int32)
    half = D // tp_count
    down_cols = down_full.reshape(down_full.shape[0], tp_count, half)
    first = cap // tp_count // 8 * 8
    main = tp_count * first
    over = -(-(cap - main) // 8) * 8

    def combine_with(back, spot):
        combine = jnp.where(
            chosen.T[None, :, :, None] & (ranks.T[None, :, :, None] == spot[:, None, None, :]),
            weight_of.T[None, :, :, None],
            0.0,
        )
        combine = jnp.moveaxis(combine, 2, 0).reshape(rows, -1)
        combine_hi = combine.astype(jnp.bfloat16)
        combine_lo = (combine - combine_hi.astype(jnp.float32)).astype(jnp.bfloat16)
        both = lax.optimization_barrier(jnp.concatenate([combine_hi, combine_lo], 0))
        parts = jnp.dot(both, back, preferred_element_type=jnp.float32)
        return parts[:rows] + parts[rows:]

    def expert_rows(arrived):
        gate_part = jnp.dot(arrived, gate_full, preferred_element_type=jnp.float32)
        up_part = jnp.dot(arrived, up_full, preferred_element_type=jnp.float32)
        return (jax.nn.silu(gate_part) * up_part).astype(jnp.bfloat16)

    def select(wanted):
        sel = chosen[:, :, None] & (ranks[:, :, None] == wanted[None, None, :])
        return sel.reshape(rows, experts * wanted.shape[0]).astype(jnp.bfloat16)

    mine = lax.dynamic_slice_in_dim(normed, tp_index * half, half, 1)
    extra = jnp.arange(main, main + over, dtype=jnp.int32)
    outgoing = jnp.einsum(
        "ts,td->sd", select(extra), mine, preferred_element_type=jnp.float32
    ).astype(jnp.bfloat16)
    arrived = lax.all_to_all(outgoing.reshape(experts, over, half), "seq", 0, 0, tiled=True)
    arrived = arrived.reshape(experts * over, half)
    partner = lax.ppermute(arrived, "tp", swap)
    arrived = jnp.where(
        tp_index == 0,
        jnp.concatenate([arrived, partner], 1),
        jnp.concatenate([partner, arrived], 1),
    )
    act = expert_rows(arrived)
    result = jnp.dot(
        act, lax.dynamic_slice_in_dim(down_cols, tp_index, 1, 1)[:, 0],
        preferred_element_type=jnp.float32,
    ).astype(jnp.bfloat16)
    back = lax.all_to_all(result.reshape(experts, over, half), "seq", 0, 0, tiled=True)
    mixture = combine_with(back.reshape(experts * over, half), extra[None, :])

    target = tp_count * jnp.arange(first, dtype=jnp.int32) + tp_index
    outgoing = jnp.einsum(
        "ts,td->sd", select(target), normed, preferred_element_type=jnp.float32
    ).astype(jnp.bfloat16)
    arrived = lax.all_to_all(
        outgoing.reshape(experts, first, D), "seq", 0, 0, tiled=True
    ).reshape(experts * first, D)
    act = expert_rows(arrived)
    result = jnp.stack(
        [
            jnp.dot(act, down_cols[:, u], preferred_element_type=jnp.float32).astype(jnp.bfloat16)
            for u in range(tp_count)
        ]
    )
    back = lax.all_to_all(
        result.reshape(tp_count * experts, first, half), ("tp", "seq"), 0, 0, tiled=True
    )
    spot = (
        tp_count * jnp.arange(first, dtype=jnp.int32)[None, :]
        + jnp.arange(tp_count, dtype=jnp.int32)[:, None]
    )
    mixture = mixture + combine_with(back.reshape(-1, half), spot)
    residual = lax.dynamic_slice_in_dim(hidden_state, tp_index * half, half, 1)
    return (residual + mixture).astype(jnp.bfloat16)


def solution(mesh):
    in_specs = (
        P("seq", None),
        P("seq", "tp"),
        P(None, "seq", "tp"),
        P(None, "seq", "tp"),
        P(),
        P("seq", None),
        P("tp", None),
        P(),
        P("seq", None),
        P("seq", None),
        P("seq", None, "tp"),
        P("seq", None, "tp"),
        P("seq", "tp", None),
    )
    out_specs = P("seq", "tp")
    return jax.shard_map(local, mesh=mesh, in_specs=in_specs, out_specs=out_specs, check_vma=False)
```

```python
import math

import jax
import jax.numpy as jnp
from jax import lax
from jax.sharding import PartitionSpec as P

D = 2048
HD = 128
TOPK = 8


def local(
    layer_input,
    query,
    suffix_kv,
    prefix_kv,
    node_len,
    path,
    out_weight,
    norm_gain,
    expert_ids,
    gates,
    w_gate,
    w_up,
    w_down,
):
    rows = query.shape[0]
    width = query.shape[1]
    heads_here = width // HD
    scale = 1.0 / math.sqrt(HD)
    seq_count = lax.axis_size("seq")
    tp_index = lax.axis_index("tp")
    tp_count = lax.axis_size("tp")
    depth = path.shape[1]
    slot = prefix_kv.shape[1]

    swap = [(i, (i + 1) % tp_count) for i in range(tp_count)]
    gate_full = jnp.concatenate([w_gate[0], lax.ppermute(w_gate[0], "tp", swap)], 1)
    up_full = jnp.concatenate([w_up[0], lax.ppermute(w_up[0], "tp", swap)], 1)
    down_full = jnp.concatenate([w_down[0], lax.ppermute(w_down[0], "tp", swap)], 0)

    pieces = prefix_kv.reshape(seq_count, -1)
    piece = pieces.shape[1]
    tag = jnp.zeros((seq_count, 128), pieces.dtype).at[:, :depth].set(
        jnp.broadcast_to(path.astype(pieces.dtype), (seq_count, depth))
    )
    outbound = jnp.concatenate([pieces, tag], 1)
    spread = lax.all_to_all(
        outbound.reshape(seq_count, -1, 128), "seq", 0, 0, tiled=True
    ).reshape(seq_count, -1)
    paths = spread[:, piece : piece + depth].astype(jnp.int32)
    spread = spread[:, :piece]
    node_ids = jnp.arange(spread.shape[0], dtype=jnp.int32)
    pick = (paths.reshape(-1)[:, None] == node_ids[None, :]).astype(spread.dtype)
    picked = jnp.dot(pick, spread, preferred_element_type=jnp.float32).astype(spread.dtype)
    got = lax.all_to_all(
        picked.reshape(seq_count, depth * piece // 128, 128), "seq", 0, 0, tiled=True
    )
    nodes_kv = got.reshape(seq_count, depth, piece).transpose(1, 0, 2).reshape(depth, 2, slot, width)
    prefix_keys = nodes_kv[:, 0].reshape(depth * slot, heads_here, HD)
    prefix_values = nodes_kv[:, 1].reshape(depth * slot, heads_here, HD)

    my_nodes = path[0]
    lengths = jnp.sum(
        jnp.where(my_nodes[:, None] == node_ids[None, :], node_len[None, :], 0), axis=1
    )
    live = (jnp.arange(slot, dtype=jnp.int32)[None, :] < lengths[:, None]).reshape(-1)
    live_all = jnp.concatenate([jnp.ones((rows,), dtype=bool), live])

    queries = query.reshape(rows, heads_here, HD)
    keys = jnp.concatenate([suffix_kv[0].reshape(rows, heads_here, HD), prefix_keys], 0)
    values = jnp.concatenate(
        [suffix_kv[1].reshape(rows, heads_here, HD), prefix_values], 0
    ).astype(jnp.float32)
    scores = (
        jnp.einsum("qhd,khd->hqk", queries, keys, preferred_element_type=jnp.float32) * scale
    )
    scores = jnp.where(live_all[None, None, :], scores, -jnp.inf)
    top = jnp.max(scores, axis=2)
    probs = jnp.exp(scores - top[:, :, None])
    total = jnp.sum(probs, axis=2)
    accum = jnp.einsum("hqk,khd->hqd", probs, values)
    attn = lax.optimization_barrier((accum / total[:, :, None]).astype(jnp.bfloat16))
    partial_value = jnp.einsum(
        "hqd,hdm->qm",
        attn,
        out_weight.reshape(heads_here, HD, D),
        preferred_element_type=jnp.float32,
    )
    heads_sum = partial_value + lax.ppermute(partial_value, "tp", swap)
    hidden_state = layer_input.astype(jnp.float32) + heads_sum
    mean_square = jnp.mean(hidden_state * hidden_state, axis=1, keepdims=True)
    normed = (hidden_state * lax.rsqrt(mean_square + 1e-06) * norm_gain).astype(jnp.bfloat16)

    experts = w_gate.shape[0] * seq_count
    cap = 5 * rows * TOPK // (4 * experts)
    hit = expert_ids[:, :, None] == jnp.arange(experts, dtype=jnp.int32)[None, None, :]
    chosen = jnp.any(hit, axis=1)
    weight_of = jnp.sum(jnp.where(hit, gates[:, :, None], 0.0), axis=1)
    token = jnp.arange(rows, dtype=jnp.int32)
    earlier = (token[None, :] < token[:, None]).astype(jnp.bfloat16)
    ranks = jnp.dot(
        earlier, chosen.astype(jnp.bfloat16), preferred_element_type=jnp.float32
    ).astype(jnp.int32)
    half = D // tp_count
    down_cols = down_full.reshape(down_full.shape[0], tp_count, half)
    first = cap // tp_count // 8 * 8
    main = tp_count * first
    over = -(-(cap - main) // 8) * 8

    def combine_with(back, spot):
        combine = jnp.where(
            chosen.T[None, :, :, None] & (ranks.T[None, :, :, None] == spot[:, None, None, :]),
            weight_of.T[None, :, :, None],
            0.0,
        )
        combine = jnp.moveaxis(combine, 2, 0).reshape(rows, -1)
        combine_hi = combine.astype(jnp.bfloat16)
        combine_lo = (combine - combine_hi.astype(jnp.float32)).astype(jnp.bfloat16)
        both = lax.optimization_barrier(jnp.concatenate([combine_hi, combine_lo], 0))
        parts = jnp.dot(both, back, preferred_element_type=jnp.float32)
        return parts[:rows] + parts[rows:]

    gate_up = jnp.concatenate([gate_full, up_full], 1)
    hidden_units = gate_full.shape[1]

    def expert_rows(arrived):
        both_parts = jnp.dot(arrived, gate_up, preferred_element_type=jnp.float32)
        gate_part = both_parts[:, :hidden_units]
        up_part = both_parts[:, hidden_units:]
        return (jax.nn.silu(gate_part) * up_part).astype(jnp.bfloat16)

    def select(wanted):
        sel = chosen[:, :, None] & (ranks[:, :, None] == wanted[None, None, :])
        return sel.reshape(rows, experts * wanted.shape[0]).astype(jnp.bfloat16)

    mine = lax.dynamic_slice_in_dim(normed, tp_index * half, half, 1)
    extra = jnp.arange(main, main + over, dtype=jnp.int32)
    outgoing = jnp.einsum(
        "ts,td->sd", select(extra), mine, preferred_element_type=jnp.float32
    ).astype(jnp.bfloat16)
    arrived = lax.all_to_all(outgoing.reshape(experts, over, half), "seq", 0, 0, tiled=True)
    arrived = arrived.reshape(experts * over, half)
    partner = lax.ppermute(arrived, "tp", swap)
    arrived = jnp.where(
        tp_index == 0,
        jnp.concatenate([arrived, partner], 1),
        jnp.concatenate([partner, arrived], 1),
    )
    act = expert_rows(arrived)
    result = jnp.dot(
        act, lax.dynamic_slice_in_dim(down_cols, tp_index, 1, 1)[:, 0],
        preferred_element_type=jnp.float32,
    ).astype(jnp.bfloat16)
    back = lax.all_to_all(result.reshape(experts, over, half), "seq", 0, 0, tiled=True)
    mixture = combine_with(back.reshape(experts * over, half), extra[None, :])

    target = tp_count * jnp.arange(first, dtype=jnp.int32) + tp_index
    outgoing = jnp.einsum(
        "ts,td->sd", select(target), normed, preferred_element_type=jnp.float32
    ).astype(jnp.bfloat16)
    arrived = lax.all_to_all(
        outgoing.reshape(experts, first, D), "seq", 0, 0, tiled=True
    ).reshape(experts * first, D)
    act = expert_rows(arrived)
    result = jnp.stack(
        [
            jnp.dot(act, down_cols[:, u], preferred_element_type=jnp.float32).astype(jnp.bfloat16)
            for u in range(tp_count)
        ]
    )
    back = lax.all_to_all(
        result.reshape(tp_count * experts, first, half), ("tp", "seq"), 0, 0, tiled=True
    )
    spot = (
        tp_count * jnp.arange(first, dtype=jnp.int32)[None, :]
        + jnp.arange(tp_count, dtype=jnp.int32)[:, None]
    )
    mixture = mixture + combine_with(back.reshape(-1, half), spot)
    residual = lax.dynamic_slice_in_dim(hidden_state, tp_index * half, half, 1)
    return (residual + mixture).astype(jnp.bfloat16)


def solution(mesh):
    in_specs = (
        P("seq", None),
        P("seq", "tp"),
        P(None, "seq", "tp"),
        P(None, "seq", "tp"),
        P(),
        P("seq", None),
        P("tp", None),
        P(),
        P("seq", None),
        P("seq", None),
        P("seq", None, "tp"),
        P("seq", None, "tp"),
        P("seq", "tp", None),
    )
    out_specs = P("seq", "tp")
    return jax.shard_map(local, mesh=mesh, in_specs=in_specs, out_specs=out_specs, check_vma=False)
```

```python
import math

import jax
import jax.numpy as jnp
from jax import lax
from jax.sharding import PartitionSpec as P

D = 2048
HD = 128
TOPK = 8


def local(
    layer_input,
    query,
    suffix_kv,
    prefix_kv,
    node_len,
    path,
    out_weight,
    norm_gain,
    expert_ids,
    gates,
    w_gate,
    w_up,
    w_down,
):
    rows = query.shape[0]
    width = query.shape[1]
    heads_here = width // HD
    scale = 1.0 / math.sqrt(HD)
    seq_count = lax.axis_size("seq")
    tp_index = lax.axis_index("tp")
    tp_count = lax.axis_size("tp")
    depth = path.shape[1]
    slot = prefix_kv.shape[1]

    swap = [(i, (i + 1) % tp_count) for i in range(tp_count)]
    gate_full = jnp.concatenate([w_gate[0], lax.ppermute(w_gate[0], "tp", swap)], 1)
    up_full = jnp.concatenate([w_up[0], lax.ppermute(w_up[0], "tp", swap)], 1)
    down_full = jnp.concatenate([w_down[0], lax.ppermute(w_down[0], "tp", swap)], 0)

    pieces = prefix_kv.reshape(seq_count, -1)
    piece = pieces.shape[1]
    tag = jnp.zeros((seq_count, 128), pieces.dtype).at[:, :depth].set(
        jnp.broadcast_to(path.astype(pieces.dtype), (seq_count, depth))
    )
    outbound = jnp.concatenate([pieces, tag], 1)
    spread = lax.all_to_all(
        outbound.reshape(seq_count, -1, 128), "seq", 0, 0, tiled=True
    ).reshape(seq_count, -1)
    paths = spread[:, piece : piece + depth].astype(jnp.int32)
    spread = spread[:, :piece]
    node_ids = jnp.arange(spread.shape[0], dtype=jnp.int32)
    pick = (paths.reshape(-1)[:, None] == node_ids[None, :]).astype(spread.dtype)
    picked = jnp.dot(pick, spread, preferred_element_type=jnp.float32).astype(spread.dtype)
    got = lax.all_to_all(
        picked.reshape(seq_count, depth * piece // 128, 128), "seq", 0, 0, tiled=True
    )
    nodes_kv = got.reshape(seq_count, depth, piece).transpose(1, 0, 2).reshape(depth, 2, slot, width)
    prefix_keys = nodes_kv[:, 0].reshape(depth * slot, heads_here, HD)
    prefix_values = nodes_kv[:, 1].reshape(depth * slot, heads_here, HD)

    my_nodes = path[0]
    lengths = jnp.sum(
        jnp.where(my_nodes[:, None] == node_ids[None, :], node_len[None, :], 0), axis=1
    )
    live = (jnp.arange(slot, dtype=jnp.int32)[None, :] < lengths[:, None]).reshape(-1)
    live_all = jnp.concatenate([jnp.ones((rows,), dtype=bool), live])

    queries = query.reshape(rows, heads_here, HD)
    keys = jnp.concatenate([suffix_kv[0].reshape(rows, heads_here, HD), prefix_keys], 0)
    values = jnp.concatenate(
        [suffix_kv[1].reshape(rows, heads_here, HD), prefix_values], 0
    ).astype(jnp.float32)
    scores = (
        jnp.einsum("qhd,khd->hqk", queries, keys, preferred_element_type=jnp.float32) * scale
    )
    scores = jnp.where(live_all[None, None, :], scores, -jnp.inf)
    top = jnp.max(scores, axis=2)
    probs = jnp.exp(scores - top[:, :, None])
    total = jnp.sum(probs, axis=2)
    accum = jnp.einsum("hqk,khd->hqd", probs, values)
    attn = lax.optimization_barrier((accum / total[:, :, None]).astype(jnp.bfloat16))
    partial_value = jnp.einsum(
        "hqd,hdm->qm",
        attn,
        out_weight.reshape(heads_here, HD, D),
        preferred_element_type=jnp.float32,
    )
    heads_sum = partial_value + lax.ppermute(partial_value, "tp", swap)
    hidden_state = layer_input.astype(jnp.float32) + heads_sum
    mean_square = jnp.mean(hidden_state * hidden_state, axis=1, keepdims=True)
    normed = (hidden_state * lax.rsqrt(mean_square + 1e-06) * norm_gain).astype(jnp.bfloat16)

    experts = w_gate.shape[0] * seq_count
    cap = 5 * rows * TOPK // (4 * experts)
    hit = expert_ids[:, :, None] == jnp.arange(experts, dtype=jnp.int32)[None, None, :]
    chosen = jnp.any(hit, axis=1)
    weight_of = jnp.sum(jnp.where(hit, gates[:, :, None], 0.0), axis=1)
    token = jnp.arange(rows, dtype=jnp.int32)
    earlier = (token[None, :] < token[:, None]).astype(jnp.bfloat16)
    ranks = jnp.dot(
        earlier, chosen.astype(jnp.bfloat16), preferred_element_type=jnp.float32
    ).astype(jnp.int32)
    half = D // tp_count
    first = cap // tp_count // 8 * 8
    main = tp_count * first
    over = -(-(cap - main) // 8) * 8

    def combine_with(back, spot):
        combine = jnp.where(
            chosen.T[None, :, :, None] & (ranks.T[None, :, :, None] == spot[:, None, None, :]),
            weight_of.T[None, :, :, None],
            0.0,
        )
        combine = jnp.moveaxis(combine, 2, 0).reshape(rows, -1)
        combine_hi = combine.astype(jnp.bfloat16)
        combine_lo = (combine - combine_hi.astype(jnp.float32)).astype(jnp.bfloat16)
        both = lax.optimization_barrier(jnp.concatenate([combine_hi, combine_lo], 0))
        parts = jnp.dot(both, back, preferred_element_type=jnp.float32)
        return parts[:rows] + parts[rows:]

    gate_up = jnp.concatenate([gate_full, up_full], 1)
    hidden_units = gate_full.shape[1]

    def expert_rows(arrived):
        both_parts = jnp.dot(arrived, gate_up, preferred_element_type=jnp.float32)
        gate_part = both_parts[:, :hidden_units]
        up_part = both_parts[:, hidden_units:]
        return (jax.nn.silu(gate_part) * up_part).astype(jnp.bfloat16)

    def select(wanted):
        sel = chosen[:, :, None] & (ranks[:, :, None] == wanted[None, None, :])
        return sel.reshape(rows, experts * wanted.shape[0]).astype(jnp.bfloat16)

    mine = lax.dynamic_slice_in_dim(normed, tp_index * half, half, 1)
    extra = jnp.arange(main, main + over, dtype=jnp.int32)
    outgoing = jnp.einsum(
        "ts,td->sd", select(extra), mine, preferred_element_type=jnp.float32
    ).astype(jnp.bfloat16)
    arrived = lax.all_to_all(outgoing.reshape(experts, over, half), "seq", 0, 0, tiled=True)
    arrived = arrived.reshape(experts * over, half)
    partner = lax.ppermute(arrived, "tp", swap)
    arrived = jnp.where(
        tp_index == 0,
        jnp.concatenate([arrived, partner], 1),
        jnp.concatenate([partner, arrived], 1),
    )
    act = expert_rows(arrived)
    result = jnp.dot(
        act, lax.dynamic_slice_in_dim(down_full, tp_index * half, half, 1),
        preferred_element_type=jnp.float32,
    ).astype(jnp.bfloat16)
    back = lax.all_to_all(result.reshape(experts, over, half), "seq", 0, 0, tiled=True)
    mixture = combine_with(back.reshape(experts * over, half), extra[None, :])

    target = tp_count * jnp.arange(first, dtype=jnp.int32) + tp_index
    outgoing = jnp.einsum(
        "ts,td->sd", select(target), normed, preferred_element_type=jnp.float32
    ).astype(jnp.bfloat16)
    arrived = lax.all_to_all(
        outgoing.reshape(experts, first, D), "seq", 0, 0, tiled=True
    ).reshape(experts * first, D)
    act = expert_rows(arrived)
    result = jnp.dot(act, down_full, preferred_element_type=jnp.float32).astype(jnp.bfloat16)
    back = lax.all_to_all(result.reshape(experts, first, D), "seq", 0, 0, tiled=True)
    partial = combine_with(back.reshape(experts * first, D), target[None, :])
    own = lax.dynamic_slice_in_dim(partial, tp_index * half, half, 1)
    theirs = lax.dynamic_slice_in_dim(partial, (tp_index + 1) % tp_count * half, half, 1)
    mixture = mixture + (own + lax.ppermute(theirs, "tp", swap))
    residual = lax.dynamic_slice_in_dim(hidden_state, tp_index * half, half, 1)
    return (residual + mixture).astype(jnp.bfloat16)


def solution(mesh):
    in_specs = (
        P("seq", None),
        P("seq", "tp"),
        P(None, "seq", "tp"),
        P(None, "seq", "tp"),
        P(),
        P("seq", None),
        P("tp", None),
        P(),
        P("seq", None),
        P("seq", None),
        P("seq", None, "tp"),
        P("seq", None, "tp"),
        P("seq", "tp", None),
    )
    out_specs = P("seq", "tp")
    return jax.shard_map(local, mesh=mesh, in_specs=in_specs, out_specs=out_specs, check_vma=False)
```

```python
import math

import jax
import jax.numpy as jnp
from jax import lax
from jax.sharding import PartitionSpec as P

D = 2048
HD = 128
TOPK = 8


def local(
    layer_input,
    query,
    suffix_kv,
    prefix_kv,
    node_len,
    path,
    out_weight,
    norm_gain,
    expert_ids,
    gates,
    w_gate,
    w_up,
    w_down,
):
    rows = query.shape[0]
    width = query.shape[1]
    heads_here = width // HD
    scale = 1.0 / math.sqrt(HD)
    seq_count = lax.axis_size("seq")
    tp_index = lax.axis_index("tp")
    tp_count = lax.axis_size("tp")
    depth = path.shape[1]
    slot = prefix_kv.shape[1]

    swap = [(i, (i + 1) % tp_count) for i in range(tp_count)]
    gate_full = jnp.concatenate([w_gate[0], lax.ppermute(w_gate[0], "tp", swap)], 1)
    up_full = jnp.concatenate([w_up[0], lax.ppermute(w_up[0], "tp", swap)], 1)
    down_full = jnp.concatenate([w_down[0], lax.ppermute(w_down[0], "tp", swap)], 0)

    pieces = prefix_kv.reshape(seq_count, -1)
    piece = pieces.shape[1]
    tag = jnp.zeros((seq_count, 128), pieces.dtype).at[:, :depth].set(
        jnp.broadcast_to(path.astype(pieces.dtype), (seq_count, depth))
    )
    outbound = jnp.concatenate([pieces, tag], 1)
    spread = lax.all_to_all(
        outbound.reshape(seq_count, -1, 128), "seq", 0, 0, tiled=True
    ).reshape(seq_count, -1)
    paths = spread[:, piece : piece + depth].astype(jnp.int32)
    spread = spread[:, :piece]
    node_ids = jnp.arange(spread.shape[0], dtype=jnp.int32)
    pick = (paths.reshape(-1)[:, None] == node_ids[None, :]).astype(spread.dtype)
    picked = jnp.dot(pick, spread, preferred_element_type=jnp.float32).astype(spread.dtype)
    got = lax.all_to_all(
        picked.reshape(seq_count, depth * piece // 128, 128), "seq", 0, 0, tiled=True
    )
    nodes_kv = got.reshape(seq_count, depth, piece).transpose(1, 0, 2).reshape(depth, 2, slot, width)
    prefix_keys = nodes_kv[:, 0].reshape(depth * slot, heads_here, HD)
    prefix_values = nodes_kv[:, 1].reshape(depth * slot, heads_here, HD)

    my_nodes = path[0]
    lengths = jnp.sum(
        jnp.where(my_nodes[:, None] == node_ids[None, :], node_len[None, :], 0), axis=1
    )
    live = (jnp.arange(slot, dtype=jnp.int32)[None, :] < lengths[:, None]).reshape(-1)
    live_all = jnp.concatenate([jnp.ones((rows,), dtype=bool), live])

    queries = query.reshape(rows, heads_here, HD)
    keys = jnp.concatenate([suffix_kv[0].reshape(rows, heads_here, HD), prefix_keys], 0)
    values = jnp.concatenate(
        [suffix_kv[1].reshape(rows, heads_here, HD), prefix_values], 0
    ).astype(jnp.float32)
    scores = (
        jnp.einsum("qhd,khd->hqk", queries, keys, preferred_element_type=jnp.float32) * scale
    )
    scores = jnp.where(live_all[None, None, :], scores, -jnp.inf)
    top = jnp.max(scores, axis=2)
    probs = jnp.exp(scores - top[:, :, None])
    total = jnp.sum(probs, axis=2)
    accum = jnp.einsum("hqk,khd->hqd", probs, values)
    attn = lax.optimization_barrier((accum / total[:, :, None]).astype(jnp.bfloat16))
    partial_value = jnp.einsum(
        "hqd,hdm->qm",
        attn,
        out_weight.reshape(heads_here, HD, D),
        preferred_element_type=jnp.float32,
    )
    heads_sum = partial_value + lax.ppermute(partial_value, "tp", swap)
    hidden_state = layer_input.astype(jnp.float32) + heads_sum
    mean_square = jnp.mean(hidden_state * hidden_state, axis=1, keepdims=True)
    normed = (hidden_state * lax.rsqrt(mean_square + 1e-06) * norm_gain).astype(jnp.bfloat16)

    experts = w_gate.shape[0] * seq_count
    cap = 5 * rows * TOPK // (4 * experts)
    hit = expert_ids[:, :, None] == jnp.arange(experts, dtype=jnp.int32)[None, None, :]
    chosen = jnp.any(hit, axis=1)
    weight_of = jnp.sum(jnp.where(hit, gates[:, :, None], 0.0), axis=1)
    token = jnp.arange(rows, dtype=jnp.int32)
    earlier = (token[None, :] < token[:, None]).astype(jnp.bfloat16)
    ranks = jnp.dot(
        earlier, chosen.astype(jnp.bfloat16), preferred_element_type=jnp.float32
    ).astype(jnp.int32)
    half = D // tp_count
    down_cols = down_full.reshape(down_full.shape[0], tp_count, half)
    first = cap // tp_count // 8 * 8
    main = tp_count * first
    over = -(-(cap - main) // 8) * 8

    def combine_with(back, spot):
        combine = jnp.where(
            chosen.T[None, :, :, None] & (ranks.T[None, :, :, None] == spot[:, None, None, :]),
            weight_of.T[None, :, :, None],
            0.0,
        )
        combine = jnp.moveaxis(combine, 2, 0).reshape(rows, -1)
        combine_hi = combine.astype(jnp.bfloat16)
        combine_lo = (combine - combine_hi.astype(jnp.float32)).astype(jnp.bfloat16)
        both = lax.optimization_barrier(jnp.concatenate([combine_hi, combine_lo], 0))
        parts = jnp.dot(both, back, preferred_element_type=jnp.float32)
        return parts[:rows] + parts[rows:]

    gate_up = jnp.concatenate([gate_full, up_full], 1)
    hidden_units = gate_full.shape[1]

    def expert_rows(arrived):
        both_parts = jnp.dot(arrived, gate_up, preferred_element_type=jnp.float32)
        gate_part = both_parts[:, :hidden_units]
        up_part = both_parts[:, hidden_units:]
        return (jax.nn.silu(gate_part) * up_part).astype(jnp.bfloat16)

    def select(wanted):
        sel = chosen[:, :, None] & (ranks[:, :, None] == wanted[None, None, :])
        return sel.reshape(rows, experts * wanted.shape[0]).astype(jnp.bfloat16)

    target = tp_count * jnp.arange(first, dtype=jnp.int32) + tp_index
    outgoing = jnp.einsum(
        "ts,td->sd", select(target), normed, preferred_element_type=jnp.float32
    ).astype(jnp.bfloat16)
    arrived = lax.all_to_all(
        outgoing.reshape(experts, first, D), "seq", 0, 0, tiled=True
    ).reshape(experts * first, D)
    arrived_main = arrived
    act = expert_rows(arrived)
    result = jnp.stack(
        [
            jnp.dot(act, down_cols[:, u], preferred_element_type=jnp.float32).astype(jnp.bfloat16)
            for u in range(tp_count)
        ]
    )
    back = lax.all_to_all(
        result.reshape(tp_count * experts, first, half), ("tp", "seq"), 0, 0, tiled=True
    )
    spot = (
        tp_count * jnp.arange(first, dtype=jnp.int32)[None, :]
        + jnp.arange(tp_count, dtype=jnp.int32)[:, None]
    )
    back_main = back
    mixture = combine_with(back.reshape(-1, half), spot)
    mine = lax.dynamic_slice_in_dim(normed, tp_index * half, half, 1)
    extra = jnp.arange(main, main + over, dtype=jnp.int32)
    outgoing = jnp.einsum(
        "ts,td->sd", select(extra), mine, preferred_element_type=jnp.float32
    ).astype(jnp.bfloat16)
    outgoing, _ = lax.optimization_barrier((outgoing, arrived_main))
    arrived = lax.all_to_all(outgoing.reshape(experts, over, half), "seq", 0, 0, tiled=True)
    arrived = arrived.reshape(experts * over, half)
    partner = lax.ppermute(arrived, "tp", swap)
    arrived = jnp.where(
        tp_index == 0,
        jnp.concatenate([arrived, partner], 1),
        jnp.concatenate([partner, arrived], 1),
    )
    act = expert_rows(arrived)
    result = jnp.dot(
        act, lax.dynamic_slice_in_dim(down_cols, tp_index, 1, 1)[:, 0],
        preferred_element_type=jnp.float32,
    ).astype(jnp.bfloat16)
    result, _ = lax.optimization_barrier((result, back_main))
    back = lax.all_to_all(result.reshape(experts, over, half), "seq", 0, 0, tiled=True)
    mixture = mixture + combine_with(back.reshape(experts * over, half), extra[None, :])

    residual = lax.dynamic_slice_in_dim(hidden_state, tp_index * half, half, 1)
    return (residual + mixture).astype(jnp.bfloat16)


def solution(mesh):
    in_specs = (
        P("seq", None),
        P("seq", "tp"),
        P(None, "seq", "tp"),
        P(None, "seq", "tp"),
        P(),
        P("seq", None),
        P("tp", None),
        P(),
        P("seq", None),
        P("seq", None),
        P("seq", None, "tp"),
        P("seq", None, "tp"),
        P("seq", "tp", None),
    )
    out_specs = P("seq", "tp")
    return jax.shard_map(local, mesh=mesh, in_specs=in_specs, out_specs=out_specs, check_vma=False)
```

```python
import math

import jax
import jax.numpy as jnp
from jax import lax
from jax.sharding import PartitionSpec as P

D = 2048
HD = 128
TOPK = 8


def local(
    layer_input,
    query,
    suffix_kv,
    prefix_kv,
    node_len,
    path,
    out_weight,
    norm_gain,
    expert_ids,
    gates,
    w_gate,
    w_up,
    w_down,
):
    rows = query.shape[0]
    width = query.shape[1]
    heads_here = width // HD
    scale = 1.0 / math.sqrt(HD)
    seq_count = lax.axis_size("seq")
    tp_index = lax.axis_index("tp")
    tp_count = lax.axis_size("tp")
    depth = path.shape[1]
    slot = prefix_kv.shape[1]

    swap = [(i, (i + 1) % tp_count) for i in range(tp_count)]
    gate_full = jnp.concatenate([w_gate[0], lax.ppermute(w_gate[0], "tp", swap)], 1)
    up_full = jnp.concatenate([w_up[0], lax.ppermute(w_up[0], "tp", swap)], 1)
    down_full = jnp.concatenate([w_down[0], lax.ppermute(w_down[0], "tp", swap)], 0)

    pieces = prefix_kv.reshape(seq_count, -1)
    piece = pieces.shape[1]
    tag = jnp.zeros((seq_count, 128), pieces.dtype).at[:, :depth].set(
        jnp.broadcast_to(path.astype(pieces.dtype), (seq_count, depth))
    )
    outbound = jnp.concatenate([pieces, tag], 1)
    spread = lax.all_to_all(
        outbound.reshape(seq_count, -1, 128), "seq", 0, 0, tiled=True
    ).reshape(seq_count, -1)
    paths = spread[:, piece : piece + depth].astype(jnp.int32)
    spread = spread[:, :piece]
    node_ids = jnp.arange(spread.shape[0], dtype=jnp.int32)
    pick = (paths.reshape(-1)[:, None] == node_ids[None, :]).astype(spread.dtype)
    picked = jnp.dot(pick, spread, preferred_element_type=jnp.float32).astype(spread.dtype)
    got = lax.all_to_all(
        picked.reshape(seq_count, depth * piece // 128, 128), "seq", 0, 0, tiled=True
    )
    nodes_kv = got.reshape(seq_count, depth, piece).transpose(1, 0, 2).reshape(depth, 2, slot, width)
    prefix_keys = nodes_kv[:, 0].reshape(depth * slot, heads_here, HD)
    prefix_values = nodes_kv[:, 1].reshape(depth * slot, heads_here, HD)

    my_nodes = path[0]
    lengths = jnp.sum(
        jnp.where(my_nodes[:, None] == node_ids[None, :], node_len[None, :], 0), axis=1
    )
    live = (jnp.arange(slot, dtype=jnp.int32)[None, :] < lengths[:, None]).reshape(-1)
    live_all = jnp.concatenate([jnp.ones((rows,), dtype=bool), live])

    queries = query.reshape(rows, heads_here, HD)
    keys = jnp.concatenate([suffix_kv[0].reshape(rows, heads_here, HD), prefix_keys], 0)
    values = jnp.concatenate(
        [suffix_kv[1].reshape(rows, heads_here, HD), prefix_values], 0
    ).astype(jnp.float32)
    scores = (
        jnp.einsum("qhd,khd->hqk", queries, keys, preferred_element_type=jnp.float32) * scale
    )
    scores = jnp.where(live_all[None, None, :], scores, -jnp.inf)
    top = jnp.max(scores, axis=2)
    probs = jnp.exp(scores - top[:, :, None])
    total = jnp.sum(probs, axis=2)
    accum = jnp.einsum("hqk,khd->hqd", probs, values)
    attn = lax.optimization_barrier((accum / total[:, :, None]).astype(jnp.bfloat16))
    partial_value = jnp.einsum(
        "hqd,hdm->qm",
        attn,
        out_weight.reshape(heads_here, HD, D),
        preferred_element_type=jnp.float32,
    )
    heads_sum = partial_value + lax.ppermute(partial_value, "tp", swap)
    hidden_state = layer_input.astype(jnp.float32) + heads_sum
    mean_square = jnp.mean(hidden_state * hidden_state, axis=1, keepdims=True)
    normed = (hidden_state * lax.rsqrt(mean_square + 1e-06) * norm_gain).astype(jnp.bfloat16)

    experts = w_gate.shape[0] * seq_count
    cap = 5 * rows * TOPK // (4 * experts)
    hit = expert_ids[:, :, None] == jnp.arange(experts, dtype=jnp.int32)[None, None, :]
    chosen = jnp.any(hit, axis=1)
    weight_of = jnp.sum(jnp.where(hit, gates[:, :, None], 0.0), axis=1)
    token = jnp.arange(rows, dtype=jnp.int32)
    earlier = (token[None, :] < token[:, None]).astype(jnp.bfloat16)
    ranks = jnp.dot(
        earlier, chosen.astype(jnp.bfloat16), preferred_element_type=jnp.float32
    ).astype(jnp.int32)
    half = D // tp_count
    down_cols = down_full.reshape(down_full.shape[0], tp_count, half)
    first = cap // tp_count // 8 * 8
    main = tp_count * first
    over = -(-(cap - main) // 8) * 8

    def combine_with(back, spot):
        combine = jnp.where(
            chosen.T[None, :, :, None] & (ranks.T[None, :, :, None] == spot[:, None, None, :]),
            weight_of.T[None, :, :, None],
            0.0,
        )
        combine = jnp.moveaxis(combine, 2, 0).reshape(rows, -1).astype(jnp.bfloat16)
        combine = lax.optimization_barrier(combine)
        return jnp.dot(combine, back, preferred_element_type=jnp.float32)

    gate_up = jnp.concatenate([gate_full, up_full], 1)
    hidden_units = gate_full.shape[1]

    def expert_rows(arrived):
        both_parts = jnp.dot(arrived, gate_up, preferred_element_type=jnp.float32)
        gate_part = both_parts[:, :hidden_units]
        up_part = both_parts[:, hidden_units:]
        return (jax.nn.silu(gate_part) * up_part).astype(jnp.bfloat16)

    def select(wanted):
        sel = chosen[:, :, None] & (ranks[:, :, None] == wanted[None, None, :])
        return sel.reshape(rows, experts * wanted.shape[0]).astype(jnp.bfloat16)

    mine = lax.dynamic_slice_in_dim(normed, tp_index * half, half, 1)
    extra = jnp.arange(main, main + over, dtype=jnp.int32)
    outgoing = jnp.einsum(
        "ts,td->sd", select(extra), mine, preferred_element_type=jnp.float32
    ).astype(jnp.bfloat16)
    arrived = lax.all_to_all(outgoing.reshape(experts, over, half), "seq", 0, 0, tiled=True)
    arrived = arrived.reshape(experts * over, half)
    partner = lax.ppermute(arrived, "tp", swap)
    arrived = jnp.where(
        tp_index == 0,
        jnp.concatenate([arrived, partner], 1),
        jnp.concatenate([partner, arrived], 1),
    )
    act = expert_rows(arrived)
    result = jnp.dot(
        act, lax.dynamic_slice_in_dim(down_cols, tp_index, 1, 1)[:, 0],
        preferred_element_type=jnp.float32,
    ).astype(jnp.bfloat16)
    back = lax.all_to_all(result.reshape(experts, over, half), "seq", 0, 0, tiled=True)
    mixture = combine_with(back.reshape(experts * over, half), extra[None, :])

    target = tp_count * jnp.arange(first, dtype=jnp.int32) + tp_index
    outgoing = jnp.einsum(
        "ts,td->sd", select(target), normed, preferred_element_type=jnp.float32
    ).astype(jnp.bfloat16)
    arrived = lax.all_to_all(
        outgoing.reshape(experts, first, D), "seq", 0, 0, tiled=True
    ).reshape(experts * first, D)
    act = expert_rows(arrived)
    result = jnp.stack(
        [
            jnp.dot(act, down_cols[:, u], preferred_element_type=jnp.float32).astype(jnp.bfloat16)
            for u in range(tp_count)
        ]
    )
    back = lax.all_to_all(
        result.reshape(tp_count * experts, first, half), ("tp", "seq"), 0, 0, tiled=True
    )
    spot = (
        tp_count * jnp.arange(first, dtype=jnp.int32)[None, :]
        + jnp.arange(tp_count, dtype=jnp.int32)[:, None]
    )
    mixture = mixture + combine_with(back.reshape(-1, half), spot)
    residual = lax.dynamic_slice_in_dim(hidden_state, tp_index * half, half, 1)
    return (residual + mixture).astype(jnp.bfloat16)


def solution(mesh):
    in_specs = (
        P("seq", None),
        P("seq", "tp"),
        P(None, "seq", "tp"),
        P(None, "seq", "tp"),
        P(),
        P("seq", None),
        P("tp", None),
        P(),
        P("seq", None),
        P("seq", None),
        P("seq", None, "tp"),
        P("seq", None, "tp"),
        P("seq", "tp", None),
    )
    out_specs = P("seq", "tp")
    return jax.shard_map(local, mesh=mesh, in_specs=in_specs, out_specs=out_specs, check_vma=False)
```

```python
import math

import jax
import jax.numpy as jnp
from jax import lax
from jax.sharding import PartitionSpec as P

D = 2048
HD = 128
TOPK = 8


def local(
    layer_input,
    query,
    suffix_kv,
    prefix_kv,
    node_len,
    path,
    out_weight,
    norm_gain,
    expert_ids,
    gates,
    w_gate,
    w_up,
    w_down,
):
    rows = query.shape[0]
    width = query.shape[1]
    heads_here = width // HD
    scale = 1.0 / math.sqrt(HD)
    seq_count = lax.axis_size("seq")
    tp_index = lax.axis_index("tp")
    tp_count = lax.axis_size("tp")
    depth = path.shape[1]
    slot = prefix_kv.shape[1]

    swap = [(i, (i + 1) % tp_count) for i in range(tp_count)]
    gate_full = jnp.concatenate([w_gate[0], lax.ppermute(w_gate[0], "tp", swap)], 1)
    up_full = jnp.concatenate([w_up[0], lax.ppermute(w_up[0], "tp", swap)], 1)
    down_full = jnp.concatenate([w_down[0], lax.ppermute(w_down[0], "tp", swap)], 0)

    pieces = prefix_kv.reshape(seq_count, -1)
    piece = pieces.shape[1]
    tag = jnp.zeros((seq_count, 128), pieces.dtype).at[:, :depth].set(
        jnp.broadcast_to(path.astype(pieces.dtype), (seq_count, depth))
    )
    outbound = jnp.concatenate([pieces, tag], 1)
    spread = lax.all_to_all(
        outbound.reshape(seq_count, -1, 128), "seq", 0, 0, tiled=True
    ).reshape(seq_count, -1)
    paths = spread[:, piece : piece + depth].astype(jnp.int32)
    spread = spread[:, :piece]
    node_ids = jnp.arange(spread.shape[0], dtype=jnp.int32)
    pick = (paths.reshape(-1)[:, None] == node_ids[None, :]).astype(spread.dtype)
    picked = jnp.dot(pick, spread, preferred_element_type=jnp.float32).astype(spread.dtype)
    got = lax.all_to_all(
        picked.reshape(seq_count, depth * piece // 128, 128), "seq", 0, 0, tiled=True
    )
    nodes_kv = got.reshape(seq_count, depth, piece).transpose(1, 0, 2).reshape(depth, 2, slot, width)
    prefix_keys = nodes_kv[:, 0].reshape(depth * slot, heads_here, HD)
    prefix_values = nodes_kv[:, 1].reshape(depth * slot, heads_here, HD)

    my_nodes = path[0]
    lengths = jnp.sum(
        jnp.where(my_nodes[:, None] == node_ids[None, :], node_len[None, :], 0), axis=1
    )
    live = (jnp.arange(slot, dtype=jnp.int32)[None, :] < lengths[:, None]).reshape(-1)
    live_all = jnp.concatenate([jnp.ones((rows,), dtype=bool), live])

    queries = query.reshape(rows, heads_here, HD)
    keys = jnp.concatenate([suffix_kv[0].reshape(rows, heads_here, HD), prefix_keys], 0)
    values = jnp.concatenate(
        [suffix_kv[1].reshape(rows, heads_here, HD), prefix_values], 0
    ).astype(jnp.float32)
    scores = (
        jnp.einsum("qhd,khd->hqk", queries, keys, preferred_element_type=jnp.float32) * scale
    )
    scores = jnp.where(live_all[None, None, :], scores, -jnp.inf)
    top = jnp.max(scores, axis=2)
    probs = jnp.exp(scores - top[:, :, None])
    total = jnp.sum(probs, axis=2)
    accum = jnp.einsum("hqk,khd->hqd", probs, values)
    attn = lax.optimization_barrier((accum / total[:, :, None]).astype(jnp.bfloat16))
    partial_value = jnp.einsum(
        "hqd,hdm->qm",
        attn,
        out_weight.reshape(heads_here, HD, D),
        preferred_element_type=jnp.float32,
    )
    heads_sum = partial_value + lax.ppermute(partial_value, "tp", swap)
    hidden_state = layer_input.astype(jnp.float32) + heads_sum
    mean_square = jnp.mean(hidden_state * hidden_state, axis=1, keepdims=True)
    normed = (hidden_state * lax.rsqrt(mean_square + 1e-06) * norm_gain).astype(jnp.bfloat16)

    experts = w_gate.shape[0] * seq_count
    cap = 5 * rows * TOPK // (4 * experts)
    hit = expert_ids[:, :, None] == jnp.arange(experts, dtype=jnp.int32)[None, None, :]
    chosen = jnp.any(hit, axis=1)
    weight_of = jnp.sum(jnp.where(hit, gates[:, :, None], 0.0), axis=1)
    token = jnp.arange(rows, dtype=jnp.int32)
    earlier = (token[None, :] < token[:, None]).astype(jnp.bfloat16)
    ranks = jnp.dot(
        earlier, chosen.astype(jnp.bfloat16), preferred_element_type=jnp.float32
    ).astype(jnp.int32)
    half = D // tp_count
    down_cols = down_full.reshape(down_full.shape[0], tp_count, half)
    first = cap // tp_count // 8 * 8
    main = tp_count * first
    over = -(-(cap - main) // 8) * 8

    def combine_with(back, spot):
        combine = jnp.where(
            chosen.T[None, :, :, None] & (ranks.T[None, :, :, None] == spot[:, None, None, :]),
            weight_of.T[None, :, :, None],
            0.0,
        )
        combine = jnp.moveaxis(combine, 2, 0).reshape(rows, -1)
        combine_hi = combine.astype(jnp.bfloat16)
        combine_lo = (combine - combine_hi.astype(jnp.float32)).astype(jnp.bfloat16)
        both = lax.optimization_barrier(jnp.concatenate([combine_hi, combine_lo], 0))
        parts = jnp.dot(both, back, preferred_element_type=jnp.float32)
        return parts[:rows] + parts[rows:]

    gate_up = jnp.concatenate([gate_full, up_full], 1)
    hidden_units = gate_full.shape[1]

    def expert_rows(arrived):
        both_parts = jnp.dot(arrived, gate_up, preferred_element_type=jnp.float32)
        gate_part = both_parts[:, :hidden_units]
        up_part = both_parts[:, hidden_units:]
        return (jax.nn.silu(gate_part) * up_part).astype(jnp.bfloat16)

    def select(wanted):
        sel = chosen[:, :, None] & (ranks[:, :, None] == wanted[None, None, :])
        return sel.reshape(rows, experts * wanted.shape[0]).astype(jnp.bfloat16)

    mine = lax.dynamic_slice_in_dim(normed, tp_index * half, half, 1)
    extra = jnp.arange(main, main + over, dtype=jnp.int32)
    outgoing = jnp.einsum(
        "ts,td->sd", select(extra), mine, preferred_element_type=jnp.float32
    ).astype(jnp.bfloat16)
    arrived = lax.all_to_all(outgoing.reshape(experts, over, half), "seq", 0, 0, tiled=True)
    arrived = arrived.reshape(experts * over, half)
    partner = lax.ppermute(arrived, "tp", swap)
    arrived = jnp.where(
        tp_index == 0,
        jnp.concatenate([arrived, partner], 1),
        jnp.concatenate([partner, arrived], 1),
    )
    act = expert_rows(arrived)
    result = jnp.dot(
        act, lax.dynamic_slice_in_dim(down_cols, tp_index, 1, 1)[:, 0],
        preferred_element_type=jnp.float32,
    ).astype(jnp.bfloat16)
    back = lax.all_to_all(result.reshape(experts, over, half), "seq", 0, 0, tiled=True)
    mixture = combine_with(back.reshape(experts * over, half), extra[None, :])

    target = tp_count * jnp.arange(first, dtype=jnp.int32) + tp_index
    outgoing = jnp.einsum(
        "ts,td->sd", select(target), normed, preferred_element_type=jnp.float32
    ).astype(jnp.bfloat16)
    arrived = lax.all_to_all(
        outgoing.reshape(experts, first, D), "seq", 0, 0, tiled=True
    ).reshape(experts * first, D)
    act = expert_rows(arrived)
    result = jnp.stack(
        [
            jnp.dot(act, down_cols[:, u], preferred_element_type=jnp.float32)
            .astype(jnp.bfloat16)
            .reshape(experts, first, half)
            for u in range(tp_count)
        ],
        axis=1,
    )
    back = lax.all_to_all(
        result.reshape(experts * tp_count, first, half), ("seq", "tp"), 0, 0, tiled=True
    )
    spot = (
        tp_count * jnp.arange(first, dtype=jnp.int32)[None, :]
        + jnp.arange(tp_count, dtype=jnp.int32)[:, None]
    )
    combine = jnp.where(
        chosen.T[:, None, :, None] & (ranks.T[:, None, :, None] == spot[None, :, None, :]),
        weight_of.T[:, None, :, None],
        0.0,
    )
    combine = jnp.moveaxis(combine, 2, 0).reshape(rows, -1)
    combine_hi = combine.astype(jnp.bfloat16)
    combine_lo = (combine - combine_hi.astype(jnp.float32)).astype(jnp.bfloat16)
    both = lax.optimization_barrier(jnp.concatenate([combine_hi, combine_lo], 0))
    parts = jnp.dot(both, back.reshape(-1, half), preferred_element_type=jnp.float32)
    mixture = mixture + (parts[:rows] + parts[rows:])
    residual = lax.dynamic_slice_in_dim(hidden_state, tp_index * half, half, 1)
    return (residual + mixture).astype(jnp.bfloat16)


def solution(mesh):
    in_specs = (
        P("seq", None),
        P("seq", "tp"),
        P(None, "seq", "tp"),
        P(None, "seq", "tp"),
        P(),
        P("seq", None),
        P("tp", None),
        P(),
        P("seq", None),
        P("seq", None),
        P("seq", None, "tp"),
        P("seq", None, "tp"),
        P("seq", "tp", None),
    )
    out_specs = P("seq", "tp")
    return jax.shard_map(local, mesh=mesh, in_specs=in_specs, out_specs=out_specs, check_vma=False)
```

```python
import math

import jax
import jax.numpy as jnp
from jax import lax
from jax.sharding import PartitionSpec as P

D = 2048
HD = 128
TOPK = 8


def local(
    layer_input,
    query,
    suffix_kv,
    prefix_kv,
    node_len,
    path,
    out_weight,
    norm_gain,
    expert_ids,
    gates,
    w_gate,
    w_up,
    w_down,
):
    rows = query.shape[0]
    width = query.shape[1]
    heads_here = width // HD
    scale = 1.0 / math.sqrt(HD)
    seq_count = lax.axis_size("seq")
    tp_index = lax.axis_index("tp")
    tp_count = lax.axis_size("tp")
    depth = path.shape[1]
    slot = prefix_kv.shape[1]

    swap = [(i, (i + 1) % tp_count) for i in range(tp_count)]
    gate_full = jnp.concatenate([w_gate[0], lax.ppermute(w_gate[0], "tp", swap)], 1)
    up_full = jnp.concatenate([w_up[0], lax.ppermute(w_up[0], "tp", swap)], 1)
    down_full = jnp.concatenate([w_down[0], lax.ppermute(w_down[0], "tp", swap)], 0)

    pieces = prefix_kv.reshape(seq_count, -1)
    piece = pieces.shape[1]
    tag = jnp.zeros((seq_count, 128), pieces.dtype).at[:, :depth].set(
        jnp.broadcast_to(path.astype(pieces.dtype), (seq_count, depth))
    )
    outbound = jnp.concatenate([pieces, tag], 1)
    spread = lax.all_to_all(
        outbound.reshape(seq_count, -1, 128), "seq", 0, 0, tiled=True
    ).reshape(seq_count, -1)
    paths = spread[:, piece : piece + depth].astype(jnp.int32)
    spread = spread[:, :piece]
    node_ids = jnp.arange(spread.shape[0], dtype=jnp.int32)
    pick = (paths.reshape(-1)[:, None] == node_ids[None, :]).astype(spread.dtype)
    picked = jnp.dot(pick, spread, preferred_element_type=jnp.float32).astype(spread.dtype)
    got = lax.all_to_all(
        picked.reshape(seq_count, depth * piece // 128, 128), "seq", 0, 0, tiled=True
    )
    nodes_kv = got.reshape(seq_count, depth, piece).transpose(1, 0, 2).reshape(depth, 2, slot, width)
    prefix_keys = nodes_kv[:, 0].reshape(depth * slot, heads_here, HD)
    prefix_values = nodes_kv[:, 1].reshape(depth * slot, heads_here, HD)

    my_nodes = path[0]
    lengths = jnp.sum(
        jnp.where(my_nodes[:, None] == node_ids[None, :], node_len[None, :], 0), axis=1
    )
    live = (jnp.arange(slot, dtype=jnp.int32)[None, :] < lengths[:, None]).reshape(-1)

    queries = query.reshape(rows, heads_here, HD)
    own_scores = (
        jnp.einsum(
            "qhd,khd->hqk",
            queries,
            suffix_kv[0].reshape(rows, heads_here, HD),
            preferred_element_type=jnp.float32,
        )
        * scale
    )
    own_top = jnp.max(own_scores, axis=2)
    own_probs = jnp.exp(own_scores - own_top[:, :, None])
    own_total = jnp.sum(own_probs, axis=2)
    own_accum = jnp.einsum(
        "hqk,khd->hqd", own_probs, suffix_kv[1].reshape(rows, heads_here, HD).astype(jnp.float32)
    )
    scores = (
        jnp.einsum("qhd,khd->hqk", queries, prefix_keys, preferred_element_type=jnp.float32)
        * scale
    )
    scores = jnp.where(live[None, None, :], scores, -jnp.inf)
    top = jnp.maximum(own_top, jnp.max(scores, axis=2))
    probs = jnp.exp(scores - top[:, :, None])
    factor = jnp.exp(own_top - top)
    total = own_total * factor + jnp.sum(probs, axis=2)
    accum = own_accum * factor[:, :, None] + jnp.einsum(
        "hqk,khd->hqd", probs, prefix_values.astype(jnp.float32)
    )
    attn = lax.optimization_barrier((accum / total[:, :, None]).astype(jnp.bfloat16))
    partial_value = jnp.einsum(
        "hqd,hdm->qm",
        attn,
        out_weight.reshape(heads_here, HD, D),
        preferred_element_type=jnp.float32,
    )
    heads_sum = partial_value + lax.ppermute(partial_value, "tp", swap)
    hidden_state = layer_input.astype(jnp.float32) + heads_sum
    mean_square = jnp.mean(hidden_state * hidden_state, axis=1, keepdims=True)
    normed = (hidden_state * lax.rsqrt(mean_square + 1e-06) * norm_gain).astype(jnp.bfloat16)

    experts = w_gate.shape[0] * seq_count
    cap = 5 * rows * TOPK // (4 * experts)
    hit = expert_ids[:, :, None] == jnp.arange(experts, dtype=jnp.int32)[None, None, :]
    chosen = jnp.any(hit, axis=1)
    weight_of = jnp.sum(jnp.where(hit, gates[:, :, None], 0.0), axis=1)
    token = jnp.arange(rows, dtype=jnp.int32)
    earlier = (token[None, :] < token[:, None]).astype(jnp.bfloat16)
    ranks = jnp.dot(
        earlier, chosen.astype(jnp.bfloat16), preferred_element_type=jnp.float32
    ).astype(jnp.int32)
    half = D // tp_count
    down_cols = down_full.reshape(down_full.shape[0], tp_count, half)
    first = cap // tp_count // 8 * 8
    main = tp_count * first
    over = -(-(cap - main) // 8) * 8

    def combine_with(back, spot):
        combine = jnp.where(
            chosen.T[None, :, :, None] & (ranks.T[None, :, :, None] == spot[:, None, None, :]),
            weight_of.T[None, :, :, None],
            0.0,
        )
        combine = jnp.moveaxis(combine, 2, 0).reshape(rows, -1)
        combine_hi = combine.astype(jnp.bfloat16)
        combine_lo = (combine - combine_hi.astype(jnp.float32)).astype(jnp.bfloat16)
        both = lax.optimization_barrier(jnp.concatenate([combine_hi, combine_lo], 0))
        parts = jnp.dot(both, back, preferred_element_type=jnp.float32)
        return parts[:rows] + parts[rows:]

    gate_up = jnp.concatenate([gate_full, up_full], 1)
    hidden_units = gate_full.shape[1]

    def expert_rows(arrived):
        both_parts = jnp.dot(arrived, gate_up, preferred_element_type=jnp.float32)
        gate_part = both_parts[:, :hidden_units]
        up_part = both_parts[:, hidden_units:]
        return (jax.nn.silu(gate_part) * up_part).astype(jnp.bfloat16)

    def select(wanted):
        sel = chosen[:, :, None] & (ranks[:, :, None] == wanted[None, None, :])
        return sel.reshape(rows, experts * wanted.shape[0]).astype(jnp.bfloat16)

    mine = lax.dynamic_slice_in_dim(normed, tp_index * half, half, 1)
    extra = jnp.arange(main, main + over, dtype=jnp.int32)
    outgoing = jnp.einsum(
        "ts,td->sd", select(extra), mine, preferred_element_type=jnp.float32
    ).astype(jnp.bfloat16)
    arrived = lax.all_to_all(outgoing.reshape(experts, over, half), "seq", 0, 0, tiled=True)
    arrived = arrived.reshape(experts * over, half)
    partner = lax.ppermute(arrived, "tp", swap)
    arrived = jnp.where(
        tp_index == 0,
        jnp.concatenate([arrived, partner], 1),
        jnp.concatenate([partner, arrived], 1),
    )
    act = expert_rows(arrived)
    result = jnp.dot(
        act, lax.dynamic_slice_in_dim(down_cols, tp_index, 1, 1)[:, 0],
        preferred_element_type=jnp.float32,
    ).astype(jnp.bfloat16)
    back = lax.all_to_all(result.reshape(experts, over, half), "seq", 0, 0, tiled=True)
    mixture = combine_with(back.reshape(experts * over, half), extra[None, :])

    target = tp_count * jnp.arange(first, dtype=jnp.int32) + tp_index
    outgoing = jnp.einsum(
        "ts,td->sd", select(target), normed, preferred_element_type=jnp.float32
    ).astype(jnp.bfloat16)
    arrived = lax.all_to_all(
        outgoing.reshape(experts, first, D), "seq", 0, 0, tiled=True
    ).reshape(experts * first, D)
    act = expert_rows(arrived)
    result = jnp.stack(
        [
            jnp.dot(act, down_cols[:, u], preferred_element_type=jnp.float32)
            .astype(jnp.bfloat16)
            .reshape(experts, first, half)
            for u in range(tp_count)
        ],
        axis=1,
    )
    back = lax.all_to_all(
        result.reshape(experts * tp_count, first, half), ("seq", "tp"), 0, 0, tiled=True
    )
    spot = (
        tp_count * jnp.arange(first, dtype=jnp.int32)[None, :]
        + jnp.arange(tp_count, dtype=jnp.int32)[:, None]
    )
    combine = jnp.where(
        chosen.T[:, None, :, None] & (ranks.T[:, None, :, None] == spot[None, :, None, :]),
        weight_of.T[:, None, :, None],
        0.0,
    )
    combine = jnp.moveaxis(combine, 2, 0).reshape(rows, -1)
    combine_hi = combine.astype(jnp.bfloat16)
    combine_lo = (combine - combine_hi.astype(jnp.float32)).astype(jnp.bfloat16)
    both = lax.optimization_barrier(jnp.concatenate([combine_hi, combine_lo], 0))
    parts = jnp.dot(both, back.reshape(-1, half), preferred_element_type=jnp.float32)
    mixture = mixture + (parts[:rows] + parts[rows:])
    residual = lax.dynamic_slice_in_dim(hidden_state, tp_index * half, half, 1)
    return (residual + mixture).astype(jnp.bfloat16)


def solution(mesh):
    in_specs = (
        P("seq", None),
        P("seq", "tp"),
        P(None, "seq", "tp"),
        P(None, "seq", "tp"),
        P(),
        P("seq", None),
        P("tp", None),
        P(),
        P("seq", None),
        P("seq", None),
        P("seq", None, "tp"),
        P("seq", None, "tp"),
        P("seq", "tp", None),
    )
    out_specs = P("seq", "tp")
    return jax.shard_map(local, mesh=mesh, in_specs=in_specs, out_specs=out_specs, check_vma=False)
```
